512 devices in a mesh: row: 32 (over z_lo, y), col: 16 (over z_hi, x, core).
Axes of the slice: x: 4, y: 4, z: 16 (z_hi: 2, z_lo: 8; z = z_hi * 8 + z_lo), core: 2. Of those that a mesh axis runs over, the one named last changes fastest.
Arguments:
- pair_act: bfloat16 [256, 256, 128], P('row', 'col'), may hold values from -6 to 6
- token_mask: int32 [256], replicated, may hold values from 0 to 1, as said below
- step_offset: int32 [1], replicated, may hold values from 0 to 65535
- triangle_weight: bfloat16 [128, 512], replicated, may hold values from -0.5 to 0.5
- query_weight: bfloat16 [128, 128], replicated, may hold values from -60 to 60
- key_value_weight: bfloat16 [128, 256], replicated, may hold values from -0.5 to 0.5
- bias_weight: bfloat16 [128, 4], replicated, may hold values from -0.5 to 0.5
- triangle_carry: float32 [256, 256, 128], P('row', 'col'), may hold values from -24 to 24
- log_carry: float32 [4, 256, 256], P(None, 'row', 'col'), may hold values from 4 to 8
- output_carry: float32 [256, 256, 128], P('row', 'col'), may hold values from -6 to 6
Outputs:
- triangle_sums: float32 [256, 256, 128], P('row', 'col')
- log_norms: float32 [4, 256, 256], P(None, 'row', 'col')
- attention_out: float32 [256, 256, 128], P('row', 'col')
The draws below stay inside these ranges and needn't reach their ends.
Inputs may be any that keep to these rules, and one draw needn't show every extreme that they name: token_mask is 1 on a leading run of tokens and 0 on a padded tail of 1 to 128 tokens. `step_offset`: only its value modulo 256 // 16 matters.
All inputs are finite; a program needn't handle non-finite values.
Results may differ from the reference program's by a relative error of at most 0.024.
The reference program's roundings to bfloat16 on the way count: a program that leaves them out, or rounds other values in their place, can miss the bound.
Values may be sent and summed in bfloat16 or wider, within the bound.
No kernel may reach another device: no remote copies, remote signals or barrier semaphores. Data moves between devices by JAX's collectives and lax.ppermute only.
A program may use at most 64 MiB of HBM per device.

```python
import math
import jax
import jax.numpy as jnp
from jax import lax

PAIR_DIM = 128
TRI_DIM = 128
HEADS = 4
HEAD_DIM = 32
TOK_BLK = 8
STEPS = 4
TOKENS = 256
N_ROW = 32
N_COL = 16


def draw_token_mask(key, part):
    length = jax.random.randint(jax.random.fold_in(key, 3), (), TOKENS // 2, TOKENS)
    return (jnp.arange(TOKENS, dtype=jnp.int32) < length).astype(jnp.int32)


def draw_query_weight(key, part):
    entries = jax.random.normal(jax.random.fold_in(key, 11), (PAIR_DIM, HEADS * HEAD_DIM), jnp.float32)
    entries = jnp.clip(entries, -4.5, 4.5) / math.sqrt(PAIR_DIM)
    return entries.astype(jnp.bfloat16)


def level_of(key, extent, pieces, least, largest):
    def one(position, parts):
        draws = jax.random.uniform(jax.random.fold_in(jax.random.fold_in(key, 6), position), (parts,), jnp.float32, least / len(pieces), largest / len(pieces))
        return jnp.repeat(jnp.exp(draws), extent[position] // parts).reshape((-1,) + (1,) * (len(extent) - position - 1))

    gain = one(*pieces[0])
    for cut in pieces[1:]:
        gain = gain * one(*cut)
    return gain


def normal_values(rng, dims, deviation, reach, cuts=(), kind=jnp.bfloat16):
    loudness = level_of(rng, dims, cuts, -0.22, 0.18) if cuts else 1.0
    values = jax.random.normal(rng, dims, jnp.float32) * deviation * loudness
    return jnp.minimum(jnp.maximum(values, -reach), reach).astype(kind)


def setup_inputs(seed: int = 0) -> dict:
    key_of = jax.random.split(jax.random.key(seed), 11)
    return {
        "pair_act": normal_values(key_of[0], (TOKENS, TOKENS, PAIR_DIM), 1.0, 6.0, ((0, 32), (1, 16))),
        "token_mask": draw_token_mask(jax.random.fold_in(key_of[10], 71), 0),
        "step_offset": jax.random.randint(key_of[2], (1,), 0, 4096 * N_COL).astype(jnp.int32),
        "triangle_weight": normal_values(key_of[3], (PAIR_DIM, 4 * TRI_DIM), PAIR_DIM ** -0.5, 0.5),
        "query_weight": draw_query_weight(jax.random.fold_in(key_of[10], 71), 0),
        "key_value_weight": normal_values(key_of[5], (PAIR_DIM, 2 * HEADS * HEAD_DIM), PAIR_DIM ** -0.5, 0.5),
        "bias_weight": normal_values(key_of[6], (PAIR_DIM, HEADS), PAIR_DIM ** -0.5, 0.5),
        "triangle_carry": normal_values(key_of[7], (TOKENS, TOKENS, TRI_DIM), 4.0, 24.0, ((0, 32), (1, 16)), jnp.float32),
        "log_carry": jnp.clip(4.0 + 4.0 * jax.random.uniform(key_of[8], (HEADS, TOKENS, TOKENS), jnp.float32) ** level_of(key_of[8], (HEADS, TOKENS, TOKENS), ((1, 32), (2, 16)), -0.2, 0.2), 4.0, 8.0),
        "output_carry": normal_values(key_of[9], (TOKENS, TOKENS, HEADS * HEAD_DIM), 1.0, 6.0, ((0, 32), (1, 16)), jnp.float32),
    }


def layer_norm(values):
    floats = values.astype(jnp.float32)
    average = lax.optimization_barrier(jnp.mean(floats, axis=-1, keepdims=True))
    centred = floats - average
    variance = lax.optimization_barrier(jnp.mean(centred * centred, axis=-1, keepdims=True))
    return (centred * lax.rsqrt(variance + 1e-05)).astype(jnp.bfloat16)

def project(normed, weight):
    flattened = normed.reshape(-1, normed.shape[-1])
    result = jnp.dot(flattened, weight, preferred_element_type=jnp.float32)
    return result.reshape(normed.shape[:-1] + (weight.shape[1],))

def gate_pair(projected, pair_keep, start):
    gate_part = projected[..., start:start + TRI_DIM]
    value_part = projected[..., start + TRI_DIM:start + 2 * TRI_DIM]
    return (jax.nn.sigmoid(gate_part) * value_part * pair_keep).astype(jnp.bfloat16)

def head_bias(normed, bias_weight):
    return jnp.transpose(project(normed, bias_weight).astype(jnp.bfloat16), (2, 0, 1))

def softmax_merge(scores, values, log_norm, outputs):
    row_max = lax.optimization_barrier(jnp.max(scores, axis=-1))
    shifted = jnp.exp(scores - row_max[..., None])
    block_log = row_max + jnp.log(lax.optimization_barrier(jnp.sum(shifted, axis=-1)))
    merged = jnp.logaddexp(log_norm, block_log)
    weights = lax.optimization_barrier(shifted.astype(jnp.bfloat16)).astype(jnp.float32)
    weighted = jnp.einsum('ihjk,ikhd->ijhd', weights, values, precision=lax.Precision.HIGHEST)
    old_scale = jnp.transpose(jnp.exp(log_norm - merged), (0, 2, 1))[..., None]
    new_scale = jnp.transpose(jnp.exp(row_max - merged), (0, 2, 1))[..., None]
    return (merged, outputs * old_scale + weighted * new_scale)

def reference(pair_act, token_mask, step_offset, triangle_weight, query_weight, key_value_weight, bias_weight, triangle_carry, log_carry, output_carry):
    tokens = TOK_BLK * N_ROW
    col_width = tokens // N_COL
    width = HEADS * HEAD_DIM
    window_width = STEPS * col_width
    starts = (step_offset[0] + jnp.arange(STEPS, dtype=jnp.int32)) % N_COL * col_width
    columns = (starts[:, None] + jnp.arange(col_width, dtype=jnp.int32)[None, :]).reshape(-1).astype(jnp.int32)
    mask_float = token_mask.astype(jnp.float32)
    key_mask = jnp.take(token_mask, columns)
    window_normed = layer_norm(jnp.take(pair_act, columns, axis=1))
    projected = project(window_normed, triangle_weight)
    pair_keep = mask_float[:, None, None] * jnp.take(mask_float, columns)[None, :, None]
    left_all = lax.optimization_barrier(gate_pair(projected, pair_keep, 0))
    right_all = lax.optimization_barrier(gate_pair(projected, pair_keep, 2 * TRI_DIM)).astype(jnp.float32)
    key_value = lax.optimization_barrier(project(window_normed, key_value_weight).astype(jnp.bfloat16))
    pair_bias = lax.optimization_barrier(head_bias(window_normed, bias_weight)).astype(jnp.float32)

    def one_block(block_items):
        rows_act, carry_rows, log_rows, out_rows, left_rows, key_rows = block_items
        summed = carry_rows
        queries = (project(layer_norm(rows_act), query_weight) * (1.0 / math.sqrt(HEAD_DIM))).astype(jnp.bfloat16)
        queries = lax.optimization_barrier(queries).astype(jnp.float32).reshape(TOK_BLK, tokens, HEADS, HEAD_DIM)
        outputs = out_rows.reshape(TOK_BLK, tokens, HEADS, HEAD_DIM)
        log_norm = log_rows
        for window_step in range(STEPS):
            col_start = window_step * col_width
            col_stop = col_start + col_width
            summed = summed + jnp.einsum('ikc,jkc->ijc', left_rows[:, col_start:col_stop].astype(jnp.float32), right_all[:, col_start:col_stop], precision=lax.Precision.HIGHEST)
            keys_part = key_rows[:, col_start:col_stop, :width].astype(jnp.float32).reshape(TOK_BLK, col_width, HEADS, HEAD_DIM)
            values_part = key_rows[:, col_start:col_stop, width:].astype(jnp.float32).reshape(TOK_BLK, col_width, HEADS, HEAD_DIM)
            scores = jnp.einsum('ijhd,ikhd->ihjk', queries, keys_part, precision=lax.Precision.HIGHEST)
            scores = scores + pair_bias[None, :, :, col_start:col_stop]
            scores = jnp.where(key_mask[col_start:col_stop][None, None, None, :] == 1, scores, -1000000000.0)
            log_norm, outputs = softmax_merge(scores, values_part, log_norm, outputs)
        return (summed, log_norm, outputs.reshape(TOK_BLK, tokens, width))
    block_inputs = (pair_act.reshape(N_ROW, TOK_BLK, tokens, PAIR_DIM), triangle_carry.reshape(N_ROW, TOK_BLK, tokens, TRI_DIM), jnp.transpose(log_carry.reshape(HEADS, N_ROW, TOK_BLK, tokens), (1, 2, 0, 3)), output_carry.reshape(N_ROW, TOK_BLK, tokens, width), left_all.reshape(N_ROW, TOK_BLK, window_width, TRI_DIM), key_value.reshape(N_ROW, TOK_BLK, window_width, 2 * width))
    summed, log_norm, outputs = lax.map(one_block, block_inputs)
    triangle_sums = summed.reshape(tokens, tokens, TRI_DIM)
    log_norms = jnp.transpose(log_norm, (2, 0, 1, 3)).reshape(HEADS, tokens, tokens)
    attention_out = outputs.reshape(tokens, tokens, width)
    return (triangle_sums, log_norms, attention_out)
```

```python
import math

import jax
import jax.numpy as jnp
from jax import lax
from jax.sharding import PartitionSpec as P

TRI_DIM = 128
HEADS = 4
HEAD_DIM = 32
STEPS = 4


def layer_norm(values):
    floats = values.astype(jnp.float32)
    average = jnp.mean(floats, axis=-1, keepdims=True)
    centred = floats - average
    variance = jnp.mean(centred * centred, axis=-1, keepdims=True)
    return (centred * lax.rsqrt(variance + 1e-05)).astype(jnp.bfloat16)


def project(normed, weight):
    flattened = normed.reshape(-1, normed.shape[-1])
    result = jnp.dot(flattened, weight, preferred_element_type=jnp.float32)
    return result.reshape(normed.shape[:-1] + (weight.shape[1],))


def gate_pair(projected, pair_keep):
    gate_part = projected[..., :TRI_DIM]
    value_part = projected[..., TRI_DIM : 2 * TRI_DIM]
    return (jax.nn.sigmoid(gate_part) * value_part * pair_keep).astype(jnp.bfloat16)


def softmax_merge(scores, values, log_norm, outputs):
    row_max = jnp.max(scores, axis=-1)
    shifted = jnp.exp(scores - row_max[..., None])
    block_log = row_max + jnp.log(jnp.sum(shifted, axis=-1))
    merged = jnp.logaddexp(log_norm, block_log)
    weights = shifted.astype(jnp.bfloat16)
    weighted = jnp.einsum("ihjk,ikhd->ijhd", weights, values, preferred_element_type=jnp.float32)
    old_scale = jnp.transpose(jnp.exp(log_norm - merged), (0, 2, 1))[..., None]
    new_scale = jnp.transpose(jnp.exp(row_max - merged), (0, 2, 1))[..., None]
    return (merged, outputs * old_scale + weighted * new_scale)


def shards(
    pair_act,
    token_mask,
    step_offset,
    triangle_weight,
    query_weight,
    key_value_weight,
    bias_weight,
    triangle_carry,
    log_carry,
    output_carry,
):
    row_count, col_width, channels = pair_act.shape
    n_row = lax.axis_size("row")
    n_col = lax.axis_size("col")
    groups = col_width // row_count
    row_index = lax.axis_index("row")
    col_index = lax.axis_index("col")
    width = HEADS * HEAD_DIM
    window = STEPS * col_width
    piece = window // n_col

    start = step_offset[0] % n_col
    block_ids = (start + jnp.arange(STEPS, dtype=jnp.int32)) % n_col
    columns = (block_ids[:, None] * col_width + jnp.arange(col_width, dtype=jnp.int32)[None, :]).reshape(-1)
    mask_float = token_mask.astype(jnp.float32)
    key_mask = jnp.take(token_mask, columns)
    key_keep = jnp.take(mask_float, columns)
    row_mask = lax.dynamic_slice_in_dim(mask_float, row_index * row_count, row_count)
    col_mask = lax.dynamic_slice_in_dim(mask_float, col_index * col_width, col_width)

    gathered = lax.all_gather(pair_act, "col", axis=1, tiled=True)
    blocks = gathered.reshape(row_count, n_col, col_width, channels)
    doubled = jnp.concatenate([blocks, blocks[:, :STEPS]], axis=1)
    rows_act = lax.dynamic_slice_in_dim(doubled, start, STEPS, axis=1).reshape(row_count, window, channels)

    mine = lax.dynamic_slice_in_dim(rows_act, col_index * piece, piece, axis=1)
    perm = [
        (src_row * n_col + src_col, ((src_row % groups) * n_col + src_col) * n_col + src_row // groups)
        for src_row in range(n_row)
        for src_col in range(n_col)
    ]
    moved = lax.ppermute(mine, ("row", "col"), perm)
    pieces = lax.all_gather(moved, "row", axis=0, tiled=False)
    cols_act = (
        pieces.reshape(groups, n_col, row_count, piece, channels)
        .transpose(0, 2, 1, 3, 4)
        .reshape(groups * row_count, window, channels)
    )

    normed = layer_norm(pair_act)
    queries = (project(normed, query_weight) * (1.0 / math.sqrt(HEAD_DIM))).astype(jnp.bfloat16)
    queries = queries.reshape(row_count, col_width, HEADS, HEAD_DIM)

    rows_normed = layer_norm(rows_act)
    cols_normed = layer_norm(cols_act)
    left = gate_pair(
        project(rows_normed, triangle_weight[:, : 2 * TRI_DIM]),
        row_mask[:, None, None] * key_keep[None, :, None],
    )
    right = gate_pair(
        project(cols_normed, triangle_weight[:, 2 * TRI_DIM :]),
        col_mask[:, None, None] * key_keep[None, :, None],
    )
    key_value = project(rows_normed, key_value_weight).astype(jnp.bfloat16)
    pair_bias = jnp.transpose(project(cols_normed, bias_weight).astype(jnp.bfloat16), (2, 0, 1))

    triangle_sums = triangle_carry + jnp.einsum(
        "ikc,jkc->ijc", left, right, preferred_element_type=jnp.float32
    )

    keys = key_value[..., :width].reshape(row_count, window, HEADS, HEAD_DIM)
    values = key_value[..., width:].reshape(row_count, window, HEADS, HEAD_DIM)
    scores = jnp.einsum("ijhd,ikhd->ihjk", queries, keys, preferred_element_type=jnp.float32)
    scores = scores + pair_bias[None].astype(jnp.float32)
    scores = jnp.where(key_mask[None, None, None, :] == 1, scores, -1000000000.0)

    log_norm = jnp.transpose(log_carry, (1, 0, 2))
    outputs = output_carry.reshape(row_count, col_width, HEADS, HEAD_DIM)
    for window_step in range(STEPS):
        lo = window_step * col_width
        hi = lo + col_width
        log_norm, outputs = softmax_merge(scores[..., lo:hi], values[:, lo:hi], log_norm, outputs)
    return (
        triangle_sums,
        jnp.transpose(log_norm, (1, 0, 2)),
        outputs.reshape(row_count, col_width, width),
    )


def solution(mesh):
    return jax.shard_map(
        shards,
        mesh=mesh,
        in_specs=(
            P("row", "col", None),
            P(),
            P(),
            P(),
            P(),
            P(),
            P(),
            P("row", "col", None),
            P(None, "row", "col"),
            P("row", "col", None),
        ),
        out_specs=(P("row", "col", None), P(None, "row", "col"), P("row", "col", None)),
        check_vma=False,
    )
```

```python
import math

import jax
import jax.numpy as jnp
from jax import lax
from jax.sharding import PartitionSpec as P

TRI_DIM = 128
HEADS = 4
HEAD_DIM = 32
STEPS = 4


def layer_norm(values):
    floats = values.astype(jnp.float32)
    average = jnp.mean(floats, axis=-1, keepdims=True)
    centred = floats - average
    variance = jnp.mean(centred * centred, axis=-1, keepdims=True)
    return (centred * lax.rsqrt(variance + 1e-05)).astype(jnp.bfloat16)


def project(normed, weight):
    flattened = normed.reshape(-1, normed.shape[-1])
    result = jnp.dot(flattened, weight, preferred_element_type=jnp.float32)
    return result.reshape(normed.shape[:-1] + (weight.shape[1],))


def gate_pair(projected, pair_keep):
    gate_part = projected[..., :TRI_DIM]
    value_part = projected[..., TRI_DIM : 2 * TRI_DIM]
    return (jax.nn.sigmoid(gate_part) * value_part * pair_keep).astype(jnp.bfloat16)


def softmax_merge(scores, values, log_norm, outputs):
    row_max = jnp.max(scores, axis=-1)
    shifted = jnp.exp(scores - row_max[..., None])
    block_log = row_max + jnp.log(jnp.sum(shifted, axis=-1))
    merged = jnp.logaddexp(log_norm, block_log)
    weights = shifted.astype(jnp.bfloat16)
    weighted = jnp.einsum("ihjk,ikhd->ijhd", weights, values, preferred_element_type=jnp.float32)
    old_scale = jnp.transpose(jnp.exp(log_norm - merged), (0, 2, 1))[..., None]
    new_scale = jnp.transpose(jnp.exp(row_max - merged), (0, 2, 1))[..., None]
    return (merged, outputs * old_scale + weighted * new_scale)


def shards(
    pair_act,
    token_mask,
    step_offset,
    triangle_weight,
    query_weight,
    key_value_weight,
    bias_weight,
    triangle_carry,
    log_carry,
    output_carry,
):
    row_count, col_width, channels = pair_act.shape
    n_row = lax.axis_size("row")
    n_col = lax.axis_size("col")
    groups = col_width // row_count
    row_index = lax.axis_index("row")
    col_index = lax.axis_index("col")
    width = HEADS * HEAD_DIM
    window = STEPS * col_width
    piece = window // n_col

    start = step_offset[0] % n_col
    block_ids = (start + jnp.arange(STEPS, dtype=jnp.int32)) % n_col
    columns = (block_ids[:, None] * col_width + jnp.arange(col_width, dtype=jnp.int32)[None, :]).reshape(-1)
    mask_float = token_mask.astype(jnp.float32)
    key_mask = jnp.take(token_mask, columns)
    key_keep = jnp.take(mask_float, columns)
    row_mask = lax.dynamic_slice_in_dim(mask_float, row_index * row_count, row_count)
    col_mask = lax.dynamic_slice_in_dim(mask_float, col_index * col_width, col_width)

    spread = jnp.broadcast_to(pair_act[None], (n_col,) + pair_act.shape)
    blocks = lax.all_to_all(spread, "col", 0, 0).transpose(1, 0, 2, 3)
    doubled = jnp.concatenate([blocks, blocks[:, :STEPS]], axis=1)
    rows_act = lax.dynamic_slice_in_dim(doubled, start, STEPS, axis=1).reshape(row_count, window, channels)

    mine = lax.dynamic_slice_in_dim(rows_act, col_index * piece, piece, axis=1)
    perm = [
        (src_row * n_col + src_col, ((src_row % groups) * n_col + src_col) * n_col + src_row // groups)
        for src_row in range(n_row)
        for src_col in range(n_col)
    ]
    moved = lax.ppermute(mine, ("row", "col"), perm)
    pieces = lax.all_to_all(jnp.broadcast_to(moved[None], (n_row,) + moved.shape), "row", 0, 0)
    cols_act = (
        pieces.reshape(groups, n_col, row_count, piece, channels)
        .transpose(0, 2, 1, 3, 4)
        .reshape(groups * row_count, window, channels)
    )

    normed = layer_norm(pair_act)
    queries = (project(normed, query_weight) * (1.0 / math.sqrt(HEAD_DIM))).astype(jnp.bfloat16)
    queries = queries.reshape(row_count, col_width, HEADS, HEAD_DIM)

    rows_normed = layer_norm(rows_act)
    cols_normed = layer_norm(cols_act)
    left = gate_pair(
        project(rows_normed, triangle_weight[:, : 2 * TRI_DIM]),
        row_mask[:, None, None] * key_keep[None, :, None],
    )
    right = gate_pair(
        project(cols_normed, triangle_weight[:, 2 * TRI_DIM :]),
        col_mask[:, None, None] * key_keep[None, :, None],
    )
    key_value = project(rows_normed, key_value_weight).astype(jnp.bfloat16)
    pair_bias = jnp.transpose(project(cols_normed, bias_weight).astype(jnp.bfloat16), (2, 0, 1))

    triangle_sums = triangle_carry + jnp.einsum(
        "ikc,jkc->ijc", left, right, preferred_element_type=jnp.float32
    )

    keys = key_value[..., :width].reshape(row_count, window, HEADS, HEAD_DIM)
    values = key_value[..., width:].reshape(row_count, window, HEADS, HEAD_DIM)
    scores = jnp.einsum("ijhd,ikhd->ihjk", queries, keys, preferred_element_type=jnp.float32)
    scores = scores + pair_bias[None].astype(jnp.float32)
    scores = jnp.where(key_mask[None, None, None, :] == 1, scores, -1000000000.0)

    log_norm = jnp.transpose(log_carry, (1, 0, 2))
    outputs = output_carry.reshape(row_count, col_width, HEADS, HEAD_DIM)
    for window_step in range(STEPS):
        lo = window_step * col_width
        hi = lo + col_width
        log_norm, outputs = softmax_merge(scores[..., lo:hi], values[:, lo:hi], log_norm, outputs)
    return (
        triangle_sums,
        jnp.transpose(log_norm, (1, 0, 2)),
        outputs.reshape(row_count, col_width, width),
    )


def solution(mesh):
    return jax.shard_map(
        shards,
        mesh=mesh,
        in_specs=(
            P("row", "col", None),
            P(),
            P(),
            P(),
            P(),
            P(),
            P(),
            P("row", "col", None),
            P(None, "row", "col"),
            P("row", "col", None),
        ),
        out_specs=(P("row", "col", None), P(None, "row", "col"), P("row", "col", None)),
        check_vma=False,
    )
```

```python
import math

import jax
import jax.numpy as jnp
from jax import lax
from jax.sharding import PartitionSpec as P

TRI_DIM = 128
HEADS = 4
HEAD_DIM = 32
STEPS = 4
COL_BITS = (3, 2, 1, 0)
ROW_BITS = (4, 3, 1, 2, 0)


def layer_norm(values):
    floats = values.astype(jnp.float32)
    average = jnp.mean(floats, axis=-1, keepdims=True)
    centred = floats - average
    variance = jnp.mean(centred * centred, axis=-1, keepdims=True)
    return (centred * lax.rsqrt(variance + 1e-05)).astype(jnp.bfloat16)


def project(normed, weight):
    flattened = normed.reshape(-1, normed.shape[-1])
    result = jnp.dot(flattened, weight, preferred_element_type=jnp.float32)
    return result.reshape(normed.shape[:-1] + (weight.shape[1],))


def gate_pair(projected, pair_keep):
    gate_part = projected[..., :TRI_DIM]
    value_part = projected[..., TRI_DIM : 2 * TRI_DIM]
    return (jax.nn.sigmoid(gate_part) * value_part * pair_keep).astype(jnp.bfloat16)


def softmax_merge(scores, values, log_norm, outputs):
    row_max = jnp.max(scores, axis=-1)
    shifted = jnp.exp(scores - row_max[..., None])
    block_log = row_max + jnp.log(jnp.sum(shifted, axis=-1))
    merged = jnp.logaddexp(log_norm, block_log)
    weights = shifted.astype(jnp.bfloat16)
    weighted = jnp.einsum("ihjk,ikhd->ijhd", weights, values, preferred_element_type=jnp.float32)
    old_scale = jnp.transpose(jnp.exp(log_norm - merged), (0, 2, 1))[..., None]
    new_scale = jnp.transpose(jnp.exp(row_max - merged), (0, 2, 1))[..., None]
    return (merged, outputs * old_scale + weighted * new_scale)


def doubling_gather(block, axis, bits):
    index = lax.axis_index(axis)
    size = lax.axis_size(axis)
    gathered = block[None]
    for bit in bits:
        stride = 1 << bit
        received = lax.ppermute(gathered, axis, [(i, i ^ stride) for i in range(size)])
        low = (index // stride) % 2 == 0
        gathered = jnp.where(low, jnp.stack([gathered, received]), jnp.stack([received, gathered]))
    order = sorted(range(len(bits)), key=lambda axis_pos: -bits[len(bits) - 1 - axis_pos])
    gathered = jnp.transpose(gathered, order + list(range(len(bits), gathered.ndim)))
    return gathered.reshape((size,) + block.shape)


def shards(
    pair_act,
    token_mask,
    step_offset,
    triangle_weight,
    query_weight,
    key_value_weight,
    bias_weight,
    triangle_carry,
    log_carry,
    output_carry,
):
    row_count, col_width, channels = pair_act.shape
    n_row = lax.axis_size("row")
    n_col = lax.axis_size("col")
    groups = col_width // row_count
    row_index = lax.axis_index("row")
    col_index = lax.axis_index("col")
    width = HEADS * HEAD_DIM
    window = STEPS * col_width
    piece = window // n_col

    start = step_offset[0] % n_col
    block_ids = (start + jnp.arange(STEPS, dtype=jnp.int32)) % n_col
    columns = (block_ids[:, None] * col_width + jnp.arange(col_width, dtype=jnp.int32)[None, :]).reshape(-1)
    mask_float = token_mask.astype(jnp.float32)
    key_mask = jnp.take(token_mask, columns)
    key_keep = jnp.take(mask_float, columns)
    row_mask = lax.dynamic_slice_in_dim(mask_float, row_index * row_count, row_count)
    col_mask = lax.dynamic_slice_in_dim(mask_float, col_index * col_width, col_width)

    blocks = doubling_gather(pair_act, "col", COL_BITS).transpose(1, 0, 2, 3)
    doubled = jnp.concatenate([blocks, blocks[:, :STEPS]], axis=1)
    rows_act = lax.dynamic_slice_in_dim(doubled, start, STEPS, axis=1).reshape(row_count, window, channels)

    mine = lax.dynamic_slice_in_dim(rows_act, col_index * piece, piece, axis=1)
    perm = [
        (src_row * n_col + src_col, ((src_row % groups) * n_col + src_col) * n_col + src_row // groups)
        for src_row in range(n_row)
        for src_col in range(n_col)
    ]
    moved = lax.ppermute(mine, ("row", "col"), perm)
    pieces = doubling_gather(moved, "row", ROW_BITS)
    cols_act = (
        pieces.reshape(groups, n_col, row_count, piece, channels)
        .transpose(0, 2, 1, 3, 4)
        .reshape(groups * row_count, window, channels)
    )

    normed = layer_norm(pair_act)
    queries = (project(normed, query_weight) * (1.0 / math.sqrt(HEAD_DIM))).astype(jnp.bfloat16)
    queries = queries.reshape(row_count, col_width, HEADS, HEAD_DIM)

    rows_normed = layer_norm(rows_act)
    cols_normed = layer_norm(cols_act)
    left = gate_pair(
        project(rows_normed, triangle_weight[:, : 2 * TRI_DIM]),
        row_mask[:, None, None] * key_keep[None, :, None],
    )
    right = gate_pair(
        project(cols_normed, triangle_weight[:, 2 * TRI_DIM :]),
        col_mask[:, None, None] * key_keep[None, :, None],
    )
    key_value = project(rows_normed, key_value_weight).astype(jnp.bfloat16)
    pair_bias = jnp.transpose(project(cols_normed, bias_weight).astype(jnp.bfloat16), (2, 0, 1))

    triangle_sums = triangle_carry + jnp.einsum(
        "ikc,jkc->ijc", left, right, preferred_element_type=jnp.float32
    )

    keys = key_value[..., :width].reshape(row_count, window, HEADS, HEAD_DIM)
    values = key_value[..., width:].reshape(row_count, window, HEADS, HEAD_DIM)
    scores = jnp.einsum("ijhd,ikhd->ihjk", queries, keys, preferred_element_type=jnp.float32)
    scores = scores + pair_bias[None].astype(jnp.float32)
    scores = jnp.where(key_mask[None, None, None, :] == 1, scores, -1000000000.0)

    log_norm = jnp.transpose(log_carry, (1, 0, 2))
    outputs = output_carry.reshape(row_count, col_width, HEADS, HEAD_DIM)
    for window_step in range(STEPS):
        lo = window_step * col_width
        hi = lo + col_width
        log_norm, outputs = softmax_merge(scores[..., lo:hi], values[:, lo:hi], log_norm, outputs)
    return (
        triangle_sums,
        jnp.transpose(log_norm, (1, 0, 2)),
        outputs.reshape(row_count, col_width, width),
    )


def solution(mesh):
    return jax.shard_map(
        shards,
        mesh=mesh,
        in_specs=(
            P("row", "col", None),
            P(),
            P(),
            P(),
            P(),
            P(),
            P(),
            P("row", "col", None),
            P(None, "row", "col"),
            P("row", "col", None),
        ),
        out_specs=(P("row", "col", None), P(None, "row", "col"), P("row", "col", None)),
        check_vma=False,
    )
```

```python
import math

import jax
import jax.numpy as jnp
from jax import lax
from jax.sharding import PartitionSpec as P

TRI_DIM = 128
HEADS = 4
HEAD_DIM = 32
STEPS = 4
COL_BITS = (3, 2, 1, 0)
ROW_BITS = (4, 3, 1, 2, 0)
Y_SIZE = 4


def layer_norm(values):
    floats = values.astype(jnp.float32)
    average = jnp.mean(floats, axis=-1, keepdims=True)
    centred = floats - average
    variance = jnp.mean(centred * centred, axis=-1, keepdims=True)
    return (centred * lax.rsqrt(variance + 1e-05)).astype(jnp.bfloat16)


def project(normed, weight):
    flattened = normed.reshape(-1, normed.shape[-1])
    result = jnp.dot(flattened, weight, preferred_element_type=jnp.float32)
    return result.reshape(normed.shape[:-1] + (weight.shape[1],))


def gate_pair(projected, pair_keep):
    gate_part = projected[..., :TRI_DIM]
    value_part = projected[..., TRI_DIM : 2 * TRI_DIM]
    return (jax.nn.sigmoid(gate_part) * value_part * pair_keep).astype(jnp.bfloat16)


def softmax_merge(scores, values, log_norm, outputs):
    row_max = jnp.max(scores, axis=-1)
    shifted = jnp.exp(scores - row_max[..., None])
    block_log = row_max + jnp.log(jnp.sum(shifted, axis=-1))
    merged = jnp.logaddexp(log_norm, block_log)
    weights = shifted.astype(jnp.bfloat16)
    weighted = jnp.einsum("ihjk,ikhd->ijhd", weights, values, preferred_element_type=jnp.float32)
    old_scale = jnp.transpose(jnp.exp(log_norm - merged), (0, 2, 1))[..., None]
    new_scale = jnp.transpose(jnp.exp(row_max - merged), (0, 2, 1))[..., None]
    return (merged, outputs * old_scale + weighted * new_scale)


def doubling_gather(block, axis, bits):
    index = lax.axis_index(axis)
    size = lax.axis_size(axis)
    gathered = block[None]
    for bit in bits:
        stride = 1 << bit
        received = lax.ppermute(gathered, axis, [(i, i ^ stride) for i in range(size)])
        low = (index // stride) % 2 == 0
        gathered = jnp.where(low, jnp.stack([gathered, received]), jnp.stack([received, gathered]))
    order = sorted(range(len(bits)), key=lambda axis_pos: -bits[len(bits) - 1 - axis_pos])
    gathered = jnp.transpose(gathered, order + list(range(len(bits), gathered.ndim)))
    return gathered.reshape((size,) + block.shape)


def grouped_gather(block, axis, outer, inner):
    inner_groups = [[g * inner + i for i in range(inner)] for g in range(outer)]
    outer_groups = [[i * inner + g for i in range(outer)] for g in range(inner)]
    spread = jnp.broadcast_to(block[None], (inner,) + block.shape)
    near = lax.all_to_all(spread, axis, 0, 0, axis_index_groups=inner_groups)
    spread = jnp.broadcast_to(near[None], (outer,) + near.shape)
    far = lax.all_to_all(spread, axis, 0, 0, axis_index_groups=outer_groups)
    return far.reshape((outer * inner,) + block.shape)


def shards(
    pair_act,
    token_mask,
    step_offset,
    triangle_weight,
    query_weight,
    key_value_weight,
    bias_weight,
    triangle_carry,
    log_carry,
    output_carry,
):
    row_count, col_width, channels = pair_act.shape
    n_row = lax.axis_size("row")
    n_col = lax.axis_size("col")
    groups = col_width // row_count
    row_index = lax.axis_index("row")
    col_index = lax.axis_index("col")
    width = HEADS * HEAD_DIM
    window = STEPS * col_width
    piece = window // n_col

    start = step_offset[0] % n_col
    block_ids = (start + jnp.arange(STEPS, dtype=jnp.int32)) % n_col
    columns = (block_ids[:, None] * col_width + jnp.arange(col_width, dtype=jnp.int32)[None, :]).reshape(-1)
    mask_float = token_mask.astype(jnp.float32)
    key_mask = jnp.take(token_mask, columns)
    key_keep = jnp.take(mask_float, columns)
    row_mask = lax.dynamic_slice_in_dim(mask_float, row_index * row_count, row_count)
    col_mask = lax.dynamic_slice_in_dim(mask_float, col_index * col_width, col_width)

    spread = jnp.broadcast_to(pair_act[None], (n_col,) + pair_act.shape)
    blocks = lax.all_to_all(spread, "col", 0, 0).transpose(1, 0, 2, 3)
    doubled = jnp.concatenate([blocks, blocks[:, :STEPS]], axis=1)
    rows_act = lax.dynamic_slice_in_dim(doubled, start, STEPS, axis=1).reshape(row_count, window, channels)

    mine = lax.dynamic_slice_in_dim(rows_act, col_index * piece, piece, axis=1)
    perm = [
        (src_row * n_col + src_col, ((src_row % groups) * n_col + src_col) * n_col + src_row // groups)
        for src_row in range(n_row)
        for src_col in range(n_col)
    ]
    moved = lax.ppermute(mine, ("row", "col"), perm)
    pieces = grouped_gather(moved, "row", n_row // Y_SIZE, Y_SIZE)
    cols_act = (
        pieces.reshape(groups, n_col, row_count, piece, channels)
        .transpose(0, 2, 1, 3, 4)
        .reshape(groups * row_count, window, channels)
    )

    normed = layer_norm(pair_act)
    queries = (project(normed, query_weight) * (1.0 / math.sqrt(HEAD_DIM))).astype(jnp.bfloat16)
    queries = queries.reshape(row_count, col_width, HEADS, HEAD_DIM)

    rows_normed = layer_norm(rows_act)
    cols_normed = layer_norm(cols_act)
    left = gate_pair(
        project(rows_normed, triangle_weight[:, : 2 * TRI_DIM]),
        row_mask[:, None, None] * key_keep[None, :, None],
    )
    right = gate_pair(
        project(cols_normed, triangle_weight[:, 2 * TRI_DIM :]),
        col_mask[:, None, None] * key_keep[None, :, None],
    )
    key_value = project(rows_normed, key_value_weight).astype(jnp.bfloat16)
    pair_bias = jnp.transpose(project(cols_normed, bias_weight).astype(jnp.bfloat16), (2, 0, 1))

    triangle_sums = triangle_carry + jnp.einsum(
        "ikc,jkc->ijc", left, right, preferred_element_type=jnp.float32
    )

    keys = key_value[..., :width].reshape(row_count, window, HEADS, HEAD_DIM)
    values = key_value[..., width:].reshape(row_count, window, HEADS, HEAD_DIM)
    scores = jnp.einsum("ijhd,ikhd->ihjk", queries, keys, preferred_element_type=jnp.float32)
    scores = scores + pair_bias[None].astype(jnp.float32)
    scores = jnp.where(key_mask[None, None, None, :] == 1, scores, -1000000000.0)

    log_norm = jnp.transpose(log_carry, (1, 0, 2))
    outputs = output_carry.reshape(row_count, col_width, HEADS, HEAD_DIM)
    for window_step in range(STEPS):
        lo = window_step * col_width
        hi = lo + col_width
        log_norm, outputs = softmax_merge(scores[..., lo:hi], values[:, lo:hi], log_norm, outputs)
    return (
        triangle_sums,
        jnp.transpose(log_norm, (1, 0, 2)),
        outputs.reshape(row_count, col_width, width),
    )


def solution(mesh):
    return jax.shard_map(
        shards,
        mesh=mesh,
        in_specs=(
            P("row", "col", None),
            P(),
            P(),
            P(),
            P(),
            P(),
            P(),
            P("row", "col", None),
            P(None, "row", "col"),
            P("row", "col", None),
        ),
        out_specs=(P("row", "col", None), P(None, "row", "col"), P("row", "col", None)),
        check_vma=False,
    )
```

```python
import math

import jax
import jax.numpy as jnp
from jax import lax
from jax.sharding import PartitionSpec as P

TRI_DIM = 128
HEADS = 4
HEAD_DIM = 32
STEPS = 4
COL_BITS = (3, 2, 1, 0)
ROW_BITS = (4, 3, 1, 2, 0)
Y_SIZE = 4


def layer_norm(values):
    floats = values.astype(jnp.float32)
    average = jnp.mean(floats, axis=-1, keepdims=True)
    centred = floats - average
    variance = jnp.mean(centred * centred, axis=-1, keepdims=True)
    return (centred * lax.rsqrt(variance + 1e-05)).astype(jnp.bfloat16)


def project(normed, weight):
    flattened = normed.reshape(-1, normed.shape[-1])
    result = jnp.dot(flattened, weight, preferred_element_type=jnp.float32)
    return result.reshape(normed.shape[:-1] + (weight.shape[1],))


def gate_pair(projected, pair_keep):
    gate_part = projected[..., :TRI_DIM]
    value_part = projected[..., TRI_DIM : 2 * TRI_DIM]
    return (jax.nn.sigmoid(gate_part) * value_part * pair_keep).astype(jnp.bfloat16)


def softmax_merge(scores, values, log_norm, outputs):
    row_max = jnp.max(scores, axis=-1)
    shifted = jnp.exp(scores - row_max[..., None])
    block_log = row_max + jnp.log(jnp.sum(shifted, axis=-1))
    merged = jnp.logaddexp(log_norm, block_log)
    weights = shifted.astype(jnp.bfloat16)
    weighted = jnp.einsum("ihjk,ikhd->ijhd", weights, values, preferred_element_type=jnp.float32)
    old_scale = jnp.transpose(jnp.exp(log_norm - merged), (0, 2, 1))[..., None]
    new_scale = jnp.transpose(jnp.exp(row_max - merged), (0, 2, 1))[..., None]
    return (merged, outputs * old_scale + weighted * new_scale)


def doubling_gather(block, axis, bits):
    index = lax.axis_index(axis)
    size = lax.axis_size(axis)
    gathered = block[None]
    for bit in bits:
        stride = 1 << bit
        received = lax.ppermute(gathered, axis, [(i, i ^ stride) for i in range(size)])
        low = (index // stride) % 2 == 0
        gathered = jnp.where(low, jnp.stack([gathered, received]), jnp.stack([received, gathered]))
    order = sorted(range(len(bits)), key=lambda axis_pos: -bits[len(bits) - 1 - axis_pos])
    gathered = jnp.transpose(gathered, order + list(range(len(bits), gathered.ndim)))
    return gathered.reshape((size,) + block.shape)


def grouped_gather(block, axis, outer, inner):
    inner_groups = [[g * inner + i for i in range(inner)] for g in range(outer)]
    outer_groups = [[i * inner + g for i in range(outer)] for g in range(inner)]
    spread = jnp.broadcast_to(block[None], (inner,) + block.shape)
    near = lax.all_to_all(spread, axis, 0, 0, axis_index_groups=inner_groups)
    spread = jnp.broadcast_to(near[None], (outer,) + near.shape)
    far = lax.all_to_all(spread, axis, 0, 0, axis_index_groups=outer_groups)
    return far.reshape((outer * inner,) + block.shape)


def shards(
    pair_act,
    token_mask,
    step_offset,
    triangle_weight,
    query_weight,
    key_value_weight,
    bias_weight,
    triangle_carry,
    log_carry,
    output_carry,
):
    row_count, col_width, channels = pair_act.shape
    n_row = lax.axis_size("row")
    n_col = lax.axis_size("col")
    groups = col_width // row_count
    row_index = lax.axis_index("row")
    col_index = lax.axis_index("col")
    width = HEADS * HEAD_DIM
    window = STEPS * col_width
    piece = window // n_col

    start = step_offset[0] % n_col
    block_ids = (start + jnp.arange(STEPS, dtype=jnp.int32)) % n_col
    columns = (block_ids[:, None] * col_width + jnp.arange(col_width, dtype=jnp.int32)[None, :]).reshape(-1)
    mask_float = token_mask.astype(jnp.float32)
    key_mask = jnp.take(token_mask, columns)
    key_keep = jnp.take(mask_float, columns)
    row_mask = lax.dynamic_slice_in_dim(mask_float, row_index * row_count, row_count)
    col_mask = lax.dynamic_slice_in_dim(mask_float, col_index * col_width, col_width)

    spread = jnp.broadcast_to(pair_act[None], (n_col,) + pair_act.shape)
    blocks = lax.all_to_all(spread, "col", 0, 0).transpose(1, 0, 2, 3)
    doubled = jnp.concatenate([blocks, blocks[:, :STEPS]], axis=1)
    rows_act = lax.dynamic_slice_in_dim(doubled, start, STEPS, axis=1).reshape(row_count, window, channels)

    mine = lax.dynamic_slice_in_dim(rows_act, col_index * piece, piece, axis=1)
    perm = [
        (src_row * n_col + src_col, ((src_row % groups) * n_col + src_col) * n_col + src_row // groups)
        for src_row in range(n_row)
        for src_col in range(n_col)
    ]
    moved = lax.ppermute(mine, ("row", "col"), perm)
    pieces = doubling_gather(moved, "row", ROW_BITS)
    cols_act = (
        pieces.reshape(groups, n_col, row_count, piece, channels)
        .transpose(0, 2, 1, 3, 4)
        .reshape(groups * row_count, window, channels)
    )

    normed = layer_norm(pair_act)
    queries = (project(normed, query_weight) * (1.0 / math.sqrt(HEAD_DIM))).astype(jnp.bfloat16)
    queries = queries.reshape(row_count, col_width, HEADS, HEAD_DIM)

    rows_normed = layer_norm(rows_act)
    cols_normed = layer_norm(cols_act)
    left = gate_pair(
        project(rows_normed, triangle_weight[:, : 2 * TRI_DIM]),
        row_mask[:, None, None] * key_keep[None, :, None],
    )
    right = gate_pair(
        project(cols_normed, triangle_weight[:, 2 * TRI_DIM :]),
        col_mask[:, None, None] * key_keep[None, :, None],
    )
    key_value = project(rows_normed, key_value_weight).astype(jnp.bfloat16)
    pair_bias = jnp.transpose(project(cols_normed, bias_weight).astype(jnp.bfloat16), (2, 0, 1))

    triangle_sums = triangle_carry + jnp.einsum(
        "ikc,jkc->ijc", left, right, preferred_element_type=jnp.float32
    )

    keys = key_value[..., :width].reshape(row_count, window, HEADS, HEAD_DIM)
    values = key_value[..., width:].reshape(row_count, window, HEADS, HEAD_DIM)
    scores = jnp.einsum("ijhd,ikhd->ihjk", queries, keys, preferred_element_type=jnp.float32)
    scores = scores + pair_bias[None].astype(jnp.float32)
    scores = jnp.where(key_mask[None, None, None, :] == 1, scores, -1000000000.0)

    log_norm = jnp.transpose(log_carry, (1, 0, 2))
    outputs = output_carry.reshape(row_count, col_width, HEADS, HEAD_DIM)
    for window_step in range(STEPS):
        lo = window_step * col_width
        hi = lo + col_width
        log_norm, outputs = softmax_merge(scores[..., lo:hi], values[:, lo:hi], log_norm, outputs)
    return (
        triangle_sums,
        jnp.transpose(log_norm, (1, 0, 2)),
        outputs.reshape(row_count, col_width, width),
    )


def solution(mesh):
    return jax.shard_map(
        shards,
        mesh=mesh,
        in_specs=(
            P("row", "col", None),
            P(),
            P(),
            P(),
            P(),
            P(),
            P(),
            P("row", "col", None),
            P(None, "row", "col"),
            P("row", "col", None),
        ),
        out_specs=(P("row", "col", None), P(None, "row", "col"), P("row", "col", None)),
        check_vma=False,
    )
```

```python
import math

import jax
import jax.numpy as jnp
from jax import lax
from jax.sharding import PartitionSpec as P

TRI_DIM = 128
HEADS = 4
HEAD_DIM = 32
STEPS = 4
COL_BITS = (3, 2, 1, 0)
ROW_BITS = (4, 3, 1, 2, 0)
Y_SIZE = 4


def layer_norm(values):
    floats = values.astype(jnp.float32)
    average = jnp.mean(floats, axis=-1, keepdims=True)
    centred = floats - average
    variance = jnp.mean(centred * centred, axis=-1, keepdims=True)
    return (centred * lax.rsqrt(variance + 1e-05)).astype(jnp.bfloat16)


def project(normed, weight):
    flattened = normed.reshape(-1, normed.shape[-1])
    result = jnp.dot(flattened, weight, preferred_element_type=jnp.float32)
    return result.reshape(normed.shape[:-1] + (weight.shape[1],))


def gate_pair(projected, pair_keep):
    gate_part = projected[..., :TRI_DIM]
    value_part = projected[..., TRI_DIM : 2 * TRI_DIM]
    return (jax.nn.sigmoid(gate_part) * value_part * pair_keep).astype(jnp.bfloat16)


def softmax_merge(scores, values, log_norm, outputs):
    row_max = jnp.max(scores, axis=-1)
    shifted = jnp.exp(scores - row_max[..., None])
    block_log = row_max + jnp.log(jnp.sum(shifted, axis=-1))
    merged = jnp.logaddexp(log_norm, block_log)
    weights = shifted.astype(jnp.bfloat16)
    weighted = jnp.einsum("ihjk,ikhd->ijhd", weights, values, preferred_element_type=jnp.float32)
    old_scale = jnp.transpose(jnp.exp(log_norm - merged), (0, 2, 1))[..., None]
    new_scale = jnp.transpose(jnp.exp(row_max - merged), (0, 2, 1))[..., None]
    return (merged, outputs * old_scale + weighted * new_scale)


def doubling_gather(block, axis, bits):
    index = lax.axis_index(axis)
    size = lax.axis_size(axis)
    gathered = block[None]
    for bit in bits:
        stride = 1 << bit
        received = lax.ppermute(gathered, axis, [(i, i ^ stride) for i in range(size)])
        low = (index // stride) % 2 == 0
        gathered = jnp.where(low, jnp.stack([gathered, received]), jnp.stack([received, gathered]))
    order = sorted(range(len(bits)), key=lambda axis_pos: -bits[len(bits) - 1 - axis_pos])
    gathered = jnp.transpose(gathered, order + list(range(len(bits), gathered.ndim)))
    return gathered.reshape((size,) + block.shape)


def grouped_gather(block, axis, outer, inner):
    inner_groups = [[g * inner + i for i in range(inner)] for g in range(outer)]
    outer_groups = [[i * inner + g for i in range(outer)] for g in range(inner)]
    spread = jnp.broadcast_to(block[None], (inner,) + block.shape)
    near = lax.all_to_all(spread, axis, 0, 0, axis_index_groups=inner_groups)
    spread = jnp.broadcast_to(near[None], (outer,) + near.shape)
    far = lax.all_to_all(spread, axis, 0, 0, axis_index_groups=outer_groups)
    return far.reshape((outer * inner,) + block.shape)


def shards(
    pair_act,
    token_mask,
    step_offset,
    triangle_weight,
    query_weight,
    key_value_weight,
    bias_weight,
    triangle_carry,
    log_carry,
    output_carry,
):
    row_count, col_width, channels = pair_act.shape
    n_row = lax.axis_size("row")
    n_col = lax.axis_size("col")
    groups = col_width // row_count
    row_index = lax.axis_index("row")
    col_index = lax.axis_index("col")
    width = HEADS * HEAD_DIM
    window = STEPS * col_width
    piece = window // n_col

    start = step_offset[0] % n_col
    block_ids = (start + jnp.arange(STEPS, dtype=jnp.int32)) % n_col
    columns = (block_ids[:, None] * col_width + jnp.arange(col_width, dtype=jnp.int32)[None, :]).reshape(-1)
    mask_float = token_mask.astype(jnp.float32)
    key_mask = jnp.take(token_mask, columns)
    key_keep = jnp.take(mask_float, columns)
    row_mask = lax.dynamic_slice_in_dim(mask_float, row_index * row_count, row_count)
    col_mask = lax.dynamic_slice_in_dim(mask_float, col_index * col_width, col_width)

    partner = lax.ppermute(pair_act, "row", [(i, i ^ 1) for i in range(n_row)])
    odd = row_index % 2 == 1
    tile = jnp.where(odd, jnp.concatenate([partner, pair_act]), jnp.concatenate([pair_act, partner]))

    def in_window(col):
        return (col - start) % n_col < STEPS

    received = lax.ppermute(tile, "col", [(i, i ^ 8) for i in range(n_col)])
    held = jnp.where(in_window(col_index), tile, received)
    mine_ok = in_window(col_index) | in_window(col_index ^ 8)
    received = lax.ppermute(held, "col", [(i, i ^ 4) for i in range(n_col)])
    held = jnp.where(mine_ok, held, received)
    received = lax.ppermute(held, "col", [(i, i ^ 2) for i in range(n_col)])
    first = ((col_index - start) % 4) // 2 == 0
    pair = jnp.where(first, jnp.stack([held, received]), jnp.stack([received, held]))
    received = lax.ppermute(pair, "col", [(i, i ^ 1) for i in range(n_col)])
    even = (col_index - start) % 2 == 0
    tiles = jnp.where(even, jnp.stack([pair, received], axis=1), jnp.stack([received, pair], axis=1))
    tiles = tiles.reshape((STEPS,) + tile.shape)

    rows_act = lax.dynamic_slice_in_dim(tiles, (row_index % groups) * row_count, row_count, axis=1)
    rows_act = rows_act.transpose(1, 0, 2, 3).reshape(row_count, window, channels)

    perm = [
        (src_row * n_col + src_col, ((src_row % groups) * n_col + src_col) * n_col + src_row // groups)
        for src_row in range(n_row)
        for src_col in range(n_col)
    ]
    moved = lax.ppermute(tiles, ("row", "col"), perm)
    cols_act = moved.transpose(1, 0, 2, 3).reshape(groups * row_count, window, channels)

    normed = layer_norm(pair_act)
    queries = (project(normed, query_weight) * (1.0 / math.sqrt(HEAD_DIM))).astype(jnp.bfloat16)
    queries = queries.reshape(row_count, col_width, HEADS, HEAD_DIM)

    rows_normed = layer_norm(rows_act)
    cols_normed = layer_norm(cols_act)
    left = gate_pair(
        project(rows_normed, triangle_weight[:, : 2 * TRI_DIM]),
        row_mask[:, None, None] * key_keep[None, :, None],
    )
    right = gate_pair(
        project(cols_normed, triangle_weight[:, 2 * TRI_DIM :]),
        col_mask[:, None, None] * key_keep[None, :, None],
    )
    key_value = project(rows_normed, key_value_weight).astype(jnp.bfloat16)
    pair_bias = jnp.transpose(project(cols_normed, bias_weight).astype(jnp.bfloat16), (2, 0, 1))

    triangle_sums = triangle_carry + jnp.einsum(
        "ikc,jkc->ijc", left, right, preferred_element_type=jnp.float32
    )

    keys = key_value[..., :width].reshape(row_count, window, HEADS, HEAD_DIM)
    values = key_value[..., width:].reshape(row_count, window, HEADS, HEAD_DIM)
    scores = jnp.einsum("ijhd,ikhd->ihjk", queries, keys, preferred_element_type=jnp.float32)
    scores = scores + pair_bias[None].astype(jnp.float32)
    scores = jnp.where(key_mask[None, None, None, :] == 1, scores, -1000000000.0)

    log_norm = jnp.transpose(log_carry, (1, 0, 2))
    outputs = output_carry.reshape(row_count, col_width, HEADS, HEAD_DIM)
    for window_step in range(STEPS):
        lo = window_step * col_width
        hi = lo + col_width
        log_norm, outputs = softmax_merge(scores[..., lo:hi], values[:, lo:hi], log_norm, outputs)
    return (
        triangle_sums,
        jnp.transpose(log_norm, (1, 0, 2)),
        outputs.reshape(row_count, col_width, width),
    )


def solution(mesh):
    return jax.shard_map(
        shards,
        mesh=mesh,
        in_specs=(
            P("row", "col", None),
            P(),
            P(),
            P(),
            P(),
            P(),
            P(),
            P("row", "col", None),
            P(None, "row", "col"),
            P("row", "col", None),
        ),
        out_specs=(P("row", "col", None), P(None, "row", "col"), P("row", "col", None)),
        check_vma=False,
    )
```

```python
import math

import jax
import jax.numpy as jnp
from jax import lax
from jax.sharding import PartitionSpec as P

TRI_DIM = 128
HEADS = 4
HEAD_DIM = 32
STEPS = 4
COL_BITS = (3, 2, 1, 0)
ROW_BITS = (4, 3, 1, 2, 0)
Y_SIZE = 4


def layer_norm(values):
    floats = values.astype(jnp.float32)
    average = jnp.mean(floats, axis=-1, keepdims=True)
    centred = floats - average
    variance = jnp.mean(centred * centred, axis=-1, keepdims=True)
    return (centred * lax.rsqrt(variance + 1e-05)).astype(jnp.bfloat16)


def project(normed, weight):
    flattened = normed.reshape(-1, normed.shape[-1])
    result = jnp.dot(flattened, weight, preferred_element_type=jnp.float32)
    return result.reshape(normed.shape[:-1] + (weight.shape[1],))


def gate_pair(projected, pair_keep):
    gate_part = projected[..., :TRI_DIM]
    value_part = projected[..., TRI_DIM : 2 * TRI_DIM]
    return (jax.nn.sigmoid(gate_part) * value_part * pair_keep).astype(jnp.bfloat16)


def softmax_merge(scores, values, log_norm, outputs):
    row_max = jnp.max(scores, axis=-1)
    shifted = jnp.exp(scores - row_max[..., None])
    block_log = row_max + jnp.log(jnp.sum(shifted, axis=-1))
    merged = jnp.logaddexp(log_norm, block_log)
    weights = shifted.astype(jnp.bfloat16)
    weighted = jnp.einsum("ihjk,ikhd->ijhd", weights, values, preferred_element_type=jnp.float32)
    old_scale = jnp.transpose(jnp.exp(log_norm - merged), (0, 2, 1))[..., None]
    new_scale = jnp.transpose(jnp.exp(row_max - merged), (0, 2, 1))[..., None]
    return (merged, outputs * old_scale + weighted * new_scale)


def doubling_gather(block, axis, bits):
    index = lax.axis_index(axis)
    size = lax.axis_size(axis)
    gathered = block[None]
    for bit in bits:
        stride = 1 << bit
        received = lax.ppermute(gathered, axis, [(i, i ^ stride) for i in range(size)])
        low = (index // stride) % 2 == 0
        gathered = jnp.where(low, jnp.stack([gathered, received]), jnp.stack([received, gathered]))
    order = sorted(range(len(bits)), key=lambda axis_pos: -bits[len(bits) - 1 - axis_pos])
    gathered = jnp.transpose(gathered, order + list(range(len(bits), gathered.ndim)))
    return gathered.reshape((size,) + block.shape)


def grouped_gather(block, axis, outer, inner):
    inner_groups = [[g * inner + i for i in range(inner)] for g in range(outer)]
    outer_groups = [[i * inner + g for i in range(outer)] for g in range(inner)]
    spread = jnp.broadcast_to(block[None], (inner,) + block.shape)
    near = lax.all_to_all(spread, axis, 0, 0, axis_index_groups=inner_groups)
    spread = jnp.broadcast_to(near[None], (outer,) + near.shape)
    far = lax.all_to_all(spread, axis, 0, 0, axis_index_groups=outer_groups)
    return far.reshape((outer * inner,) + block.shape)


def chip_position(row, col):
    return ((col // 2) % 4, row % 4, 8 * (col // 8) + row // 4)


def hop_count(source, target):
    sizes = (4, 4, 16)
    total = 0
    for a, b, n in zip(source, target, sizes):
        d = abs(a - b) % n
        total += min(d, n - d)
    return total


def assignment(cost):
    n = len(cost)
    u = [0] * (n + 1)
    v = [0] * (n + 1)
    match = [0] * (n + 1)
    way = [0] * (n + 1)
    for i in range(1, n + 1):
        match[0] = i
        j0 = 0
        minv = [float("inf")] * (n + 1)
        used = [False] * (n + 1)
        while True:
            used[j0] = True
            i0 = match[j0]
            delta = float("inf")
            j1 = 0
            for j in range(1, n + 1):
                if not used[j]:
                    cur = cost[i0 - 1][j - 1] - u[i0] - v[j]
                    if cur < minv[j]:
                        minv[j] = cur
                        way[j] = j0
                    if minv[j] < delta:
                        delta = minv[j]
                        j1 = j
            for j in range(n + 1):
                if used[j]:
                    u[match[j]] += delta
                    v[j] -= delta
                else:
                    minv[j] -= delta
            j0 = j1
            if match[j0] == 0:
                break
        while True:
            j1 = way[j0]
            match[j0] = match[j1]
            j0 = j1
            if j0 == 0:
                break
    chosen = [0] * n
    for j in range(1, n + 1):
        chosen[match[j] - 1] = j - 1
    return chosen


def owner_perm(n_row, n_col, groups):
    perm = []
    for col in range(n_col):
        sources = [(r, cc) for r in range(groups * col, groups * col + groups) for cc in range(n_col)]
        cost = [
            [hop_count(chip_position(*src), chip_position(p, col)) ** 2 for p in range(n_row)]
            for src in sources
        ]
        for src, p in zip(sources, assignment(cost)):
            perm.append((src[0] * n_col + src[1], p * n_col + col))
    return perm


def shards(
    pair_act,
    token_mask,
    step_offset,
    triangle_weight,
    query_weight,
    key_value_weight,
    bias_weight,
    triangle_carry,
    log_carry,
    output_carry,
):
    row_count, col_width, channels = pair_act.shape
    n_row = lax.axis_size("row")
    n_col = lax.axis_size("col")
    groups = col_width // row_count
    row_index = lax.axis_index("row")
    col_index = lax.axis_index("col")
    width = HEADS * HEAD_DIM
    window = STEPS * col_width
    piece = window // n_col

    start = step_offset[0] % n_col
    block_ids = (start + jnp.arange(STEPS, dtype=jnp.int32)) % n_col
    columns = (block_ids[:, None] * col_width + jnp.arange(col_width, dtype=jnp.int32)[None, :]).reshape(-1)
    mask_float = token_mask.astype(jnp.float32)
    key_mask = jnp.take(token_mask, columns)
    key_keep = jnp.take(mask_float, columns)
    row_mask = lax.dynamic_slice_in_dim(mask_float, row_index * row_count, row_count)
    col_mask = lax.dynamic_slice_in_dim(mask_float, col_index * col_width, col_width)

    partner = lax.ppermute(pair_act, "row", [(i, i ^ 1) for i in range(n_row)])
    odd = row_index % 2 == 1
    tile = jnp.where(odd, jnp.concatenate([partner, pair_act]), jnp.concatenate([pair_act, partner]))

    def in_window(col):
        return (col - start) % n_col < STEPS

    received = lax.ppermute(tile, "col", [(i, i ^ 8) for i in range(n_col)])
    held = jnp.where(in_window(col_index), tile, received)
    mine_ok = in_window(col_index) | in_window(col_index ^ 8)
    received = lax.ppermute(held, "col", [(i, i ^ 4) for i in range(n_col)])
    held = jnp.where(mine_ok, held, received)
    received = lax.ppermute(held, "col", [(i, i ^ 2) for i in range(n_col)])
    first = ((col_index - start) % 4) // 2 == 0
    pair = jnp.where(first, jnp.stack([held, received]), jnp.stack([received, held]))
    received = lax.ppermute(pair, "col", [(i, i ^ 1) for i in range(n_col)])
    even = (col_index - start) % 2 == 0
    tiles = jnp.where(even, jnp.stack([pair, received], axis=1), jnp.stack([received, pair], axis=1))
    tiles = tiles.reshape((STEPS,) + tile.shape)

    rows_act = lax.dynamic_slice_in_dim(tiles, (row_index % groups) * row_count, row_count, axis=1)
    rows_act = rows_act.transpose(1, 0, 2, 3).reshape(row_count, window, channels)

    perm = owner_perm(n_row, n_col, groups)
    moved = lax.ppermute(tiles, ("row", "col"), perm)
    cols_act = moved.transpose(1, 0, 2, 3).reshape(groups * row_count, window, channels)

    normed = layer_norm(pair_act)
    queries = (project(normed, query_weight) * (1.0 / math.sqrt(HEAD_DIM))).astype(jnp.bfloat16)
    queries = queries.reshape(row_count, col_width, HEADS, HEAD_DIM)

    rows_normed = layer_norm(rows_act)
    cols_normed = layer_norm(cols_act)
    left = gate_pair(
        project(rows_normed, triangle_weight[:, : 2 * TRI_DIM]),
        row_mask[:, None, None] * key_keep[None, :, None],
    )
    right = gate_pair(
        project(cols_normed, triangle_weight[:, 2 * TRI_DIM :]),
        col_mask[:, None, None] * key_keep[None, :, None],
    )
    key_value = project(rows_normed, key_value_weight).astype(jnp.bfloat16)
    pair_bias = jnp.transpose(project(cols_normed, bias_weight).astype(jnp.bfloat16), (2, 0, 1))

    triangle_sums = triangle_carry + jnp.einsum(
        "ikc,jkc->ijc", left, right, preferred_element_type=jnp.float32
    )

    keys = key_value[..., :width].reshape(row_count, window, HEADS, HEAD_DIM)
    values = key_value[..., width:].reshape(row_count, window, HEADS, HEAD_DIM)
    scores = jnp.einsum("ijhd,ikhd->ihjk", queries, keys, preferred_element_type=jnp.float32)
    scores = scores + pair_bias[None].astype(jnp.float32)
    scores = jnp.where(key_mask[None, None, None, :] == 1, scores, -1000000000.0)

    log_norm = jnp.transpose(log_carry, (1, 0, 2))
    outputs = output_carry.reshape(row_count, col_width, HEADS, HEAD_DIM)
    for window_step in range(STEPS):
        lo = window_step * col_width
        hi = lo + col_width
        log_norm, outputs = softmax_merge(scores[..., lo:hi], values[:, lo:hi], log_norm, outputs)
    return (
        triangle_sums,
        jnp.transpose(log_norm, (1, 0, 2)),
        outputs.reshape(row_count, col_width, width),
    )


def solution(mesh):
    return jax.shard_map(
        shards,
        mesh=mesh,
        in_specs=(
            P("row", "col", None),
            P(),
            P(),
            P(),
            P(),
            P(),
            P(),
            P("row", "col", None),
            P(None, "row", "col"),
            P("row", "col", None),
        ),
        out_specs=(P("row", "col", None), P(None, "row", "col"), P("row", "col", None)),
        check_vma=False,
    )
```

```python
import math

import jax
import jax.numpy as jnp
from jax import lax
from jax.sharding import PartitionSpec as P

TRI_DIM = 128
HEADS = 4
HEAD_DIM = 32
STEPS = 4
COL_BITS = (3, 2, 1, 0)
ROW_BITS = (4, 3, 1, 2, 0)
Y_SIZE = 4


def layer_norm(values):
    floats = values.astype(jnp.float32)
    average = jnp.mean(floats, axis=-1, keepdims=True)
    centred = floats - average
    variance = jnp.mean(centred * centred, axis=-1, keepdims=True)
    return (centred * lax.rsqrt(variance + 1e-05)).astype(jnp.bfloat16)


def project(normed, weight):
    flattened = normed.reshape(-1, normed.shape[-1])
    result = jnp.dot(flattened, weight, preferred_element_type=jnp.float32)
    return result.reshape(normed.shape[:-1] + (weight.shape[1],))


def gate_pair(projected, pair_keep):
    gate_part = projected[..., :TRI_DIM]
    value_part = projected[..., TRI_DIM : 2 * TRI_DIM]
    return (jax.nn.sigmoid(gate_part) * value_part * pair_keep).astype(jnp.bfloat16)


def softmax_merge(scores, values, log_norm, outputs):
    row_max = jnp.max(scores, axis=-1)
    shifted = jnp.exp(scores - row_max[..., None])
    block_log = row_max + jnp.log(jnp.sum(shifted, axis=-1))
    merged = jnp.logaddexp(log_norm, block_log)
    weights = shifted.astype(jnp.bfloat16)
    weighted = jnp.einsum("ihjk,ikhd->ijhd", weights, values, preferred_element_type=jnp.float32)
    old_scale = jnp.transpose(jnp.exp(log_norm - merged), (0, 2, 1))[..., None]
    new_scale = jnp.transpose(jnp.exp(row_max - merged), (0, 2, 1))[..., None]
    return (merged, outputs * old_scale + weighted * new_scale)


def doubling_gather(block, axis, bits):
    index = lax.axis_index(axis)
    size = lax.axis_size(axis)
    gathered = block[None]
    for bit in bits:
        stride = 1 << bit
        received = lax.ppermute(gathered, axis, [(i, i ^ stride) for i in range(size)])
        low = (index // stride) % 2 == 0
        gathered = jnp.where(low, jnp.stack([gathered, received]), jnp.stack([received, gathered]))
    order = sorted(range(len(bits)), key=lambda axis_pos: -bits[len(bits) - 1 - axis_pos])
    gathered = jnp.transpose(gathered, order + list(range(len(bits), gathered.ndim)))
    return gathered.reshape((size,) + block.shape)


def grouped_gather(block, axis, outer, inner):
    inner_groups = [[g * inner + i for i in range(inner)] for g in range(outer)]
    outer_groups = [[i * inner + g for i in range(outer)] for g in range(inner)]
    spread = jnp.broadcast_to(block[None], (inner,) + block.shape)
    near = lax.all_to_all(spread, axis, 0, 0, axis_index_groups=inner_groups)
    spread = jnp.broadcast_to(near[None], (outer,) + near.shape)
    far = lax.all_to_all(spread, axis, 0, 0, axis_index_groups=outer_groups)
    return far.reshape((outer * inner,) + block.shape)


def chip_position(row, col):
    return ((col // 2) % 4, row % 4, 8 * (col // 8) + row // 4)


def hop_count(source, target):
    sizes = (4, 4, 16)
    total = 0
    for a, b, n in zip(source, target, sizes):
        d = abs(a - b) % n
        total += min(d, n - d)
    return total


def assignment(cost):
    n = len(cost)
    u = [0] * (n + 1)
    v = [0] * (n + 1)
    match = [0] * (n + 1)
    way = [0] * (n + 1)
    for i in range(1, n + 1):
        match[0] = i
        j0 = 0
        minv = [float("inf")] * (n + 1)
        used = [False] * (n + 1)
        while True:
            used[j0] = True
            i0 = match[j0]
            delta = float("inf")
            j1 = 0
            for j in range(1, n + 1):
                if not used[j]:
                    cur = cost[i0 - 1][j - 1] - u[i0] - v[j]
                    if cur < minv[j]:
                        minv[j] = cur
                        way[j] = j0
                    if minv[j] < delta:
                        delta = minv[j]
                        j1 = j
            for j in range(n + 1):
                if used[j]:
                    u[match[j]] += delta
                    v[j] -= delta
                else:
                    minv[j] -= delta
            j0 = j1
            if match[j0] == 0:
                break
        while True:
            j1 = way[j0]
            match[j0] = match[j1]
            j0 = j1
            if j0 == 0:
                break
    chosen = [0] * n
    for j in range(1, n + 1):
        chosen[match[j] - 1] = j - 1
    return chosen


def owner_perm(n_row, n_col, groups):
    perm = []
    for col in range(n_col):
        sources = [(r, cc) for r in range(groups * col, groups * col + groups) for cc in range(n_col)]
        cost = [
            [hop_count(chip_position(*src), chip_position(p, col)) ** 2 for p in range(n_row)]
            for src in sources
        ]
        for src, p in zip(sources, assignment(cost)):
            perm.append((src[0] * n_col + src[1], p * n_col + col))
    return perm


def shards(
    pair_act,
    token_mask,
    step_offset,
    triangle_weight,
    query_weight,
    key_value_weight,
    bias_weight,
    triangle_carry,
    log_carry,
    output_carry,
):
    row_count, col_width, channels = pair_act.shape
    n_row = lax.axis_size("row")
    n_col = lax.axis_size("col")
    groups = col_width // row_count
    row_index = lax.axis_index("row")
    col_index = lax.axis_index("col")
    width = HEADS * HEAD_DIM
    window = STEPS * col_width
    piece = window // n_col

    start = step_offset[0] % n_col
    block_ids = (start + jnp.arange(STEPS, dtype=jnp.int32)) % n_col
    columns = (block_ids[:, None] * col_width + jnp.arange(col_width, dtype=jnp.int32)[None, :]).reshape(-1)
    mask_float = token_mask.astype(jnp.float32)
    key_mask = jnp.take(token_mask, columns)
    key_keep = jnp.take(mask_float, columns)
    row_mask = lax.dynamic_slice_in_dim(mask_float, row_index * row_count, row_count)
    col_mask = lax.dynamic_slice_in_dim(mask_float, col_index * col_width, col_width)

    def in_window(col):
        return (col - start) % n_col < STEPS

    received = lax.ppermute(pair_act, "col", [(i, i ^ 8) for i in range(n_col)])
    held = jnp.where(in_window(col_index), pair_act, received)
    mine_ok = in_window(col_index) | in_window(col_index ^ 8)

    partner = lax.ppermute(held, "row", [(i, i ^ 1) for i in range(n_row)])
    odd = row_index % 2 == 1
    held = jnp.where(odd, jnp.concatenate([partner, held]), jnp.concatenate([held, partner]))

    received = lax.ppermute(held, "col", [(i, i ^ 4) for i in range(n_col)])
    held = jnp.where(mine_ok, held, received)
    received = lax.ppermute(held, "col", [(i, i ^ 2) for i in range(n_col)])
    first = ((col_index - start) % 4) // 2 == 0
    pair = jnp.where(first, jnp.stack([held, received]), jnp.stack([received, held]))
    received = lax.ppermute(pair, "col", [(i, i ^ 1) for i in range(n_col)])
    even = (col_index - start) % 2 == 0
    tiles = jnp.where(even, jnp.stack([pair, received], axis=1), jnp.stack([received, pair], axis=1))
    tiles = tiles.reshape((STEPS,) + held.shape)

    rows_act = lax.dynamic_slice_in_dim(tiles, (row_index % groups) * row_count, row_count, axis=1)
    rows_act = rows_act.transpose(1, 0, 2, 3).reshape(row_count, window, channels)

    perm = owner_perm(n_row, n_col, groups)
    moved = lax.ppermute(tiles, ("row", "col"), perm)
    cols_act = moved.transpose(1, 0, 2, 3).reshape(groups * row_count, window, channels)

    normed = layer_norm(pair_act)
    queries = (project(normed, query_weight) * (1.0 / math.sqrt(HEAD_DIM))).astype(jnp.bfloat16)
    queries = queries.reshape(row_count, col_width, HEADS, HEAD_DIM)

    rows_normed = layer_norm(rows_act)
    cols_normed = layer_norm(cols_act)
    left = gate_pair(
        project(rows_normed, triangle_weight[:, : 2 * TRI_DIM]),
        row_mask[:, None, None] * key_keep[None, :, None],
    )
    right = gate_pair(
        project(cols_normed, triangle_weight[:, 2 * TRI_DIM :]),
        col_mask[:, None, None] * key_keep[None, :, None],
    )
    key_value = project(rows_normed, key_value_weight).astype(jnp.bfloat16)
    pair_bias = jnp.transpose(project(cols_normed, bias_weight).astype(jnp.bfloat16), (2, 0, 1))

    triangle_sums = triangle_carry + jnp.einsum(
        "ikc,jkc->ijc", left, right, preferred_element_type=jnp.float32
    )

    keys = key_value[..., :width].reshape(row_count, window, HEADS, HEAD_DIM)
    values = key_value[..., width:].reshape(row_count, window, HEADS, HEAD_DIM)
    scores = jnp.einsum("ijhd,ikhd->ihjk", queries, keys, preferred_element_type=jnp.float32)
    scores = scores + pair_bias[None].astype(jnp.float32)
    scores = jnp.where(key_mask[None, None, None, :] == 1, scores, -1000000000.0)

    log_norm = jnp.transpose(log_carry, (1, 0, 2))
    outputs = output_carry.reshape(row_count, col_width, HEADS, HEAD_DIM)
    for window_step in range(STEPS):
        lo = window_step * col_width
        hi = lo + col_width
        log_norm, outputs = softmax_merge(scores[..., lo:hi], values[:, lo:hi], log_norm, outputs)
    return (
        triangle_sums,
        jnp.transpose(log_norm, (1, 0, 2)),
        outputs.reshape(row_count, col_width, width),
    )


def solution(mesh):
    return jax.shard_map(
        shards,
        mesh=mesh,
        in_specs=(
            P("row", "col", None),
            P(),
            P(),
            P(),
            P(),
            P(),
            P(),
            P("row", "col", None),
            P(None, "row", "col"),
            P("row", "col", None),
        ),
        out_specs=(P("row", "col", None), P(None, "row", "col"), P("row", "col", None)),
        check_vma=False,
    )
```

```python
import collections
import itertools
import math

import jax
import jax.numpy as jnp
from jax import lax
from jax.sharding import PartitionSpec as P

TRI_DIM = 128
HEADS = 4
HEAD_DIM = 32
STEPS = 4
COL_BITS = (3, 2, 1, 0)
ROW_BITS = (4, 3, 1, 2, 0)
Y_SIZE = 4


def layer_norm(values):
    floats = values.astype(jnp.float32)
    average = jnp.mean(floats, axis=-1, keepdims=True)
    centred = floats - average
    variance = jnp.mean(centred * centred, axis=-1, keepdims=True)
    return (centred * lax.rsqrt(variance + 1e-05)).astype(jnp.bfloat16)


def project(normed, weight):
    flattened = normed.reshape(-1, normed.shape[-1])
    result = jnp.dot(flattened, weight, preferred_element_type=jnp.float32)
    return result.reshape(normed.shape[:-1] + (weight.shape[1],))


def gate_pair(projected, pair_keep):
    gate_part = projected[..., :TRI_DIM]
    value_part = projected[..., TRI_DIM : 2 * TRI_DIM]
    return (jax.nn.sigmoid(gate_part) * value_part * pair_keep).astype(jnp.bfloat16)


def softmax_merge(scores, values, log_norm, outputs):
    row_max = jnp.max(scores, axis=-1)
    shifted = jnp.exp(scores - row_max[..., None])
    block_log = row_max + jnp.log(jnp.sum(shifted, axis=-1))
    merged = jnp.logaddexp(log_norm, block_log)
    weights = shifted.astype(jnp.bfloat16)
    weighted = jnp.einsum("ihjk,ikhd->ijhd", weights, values, preferred_element_type=jnp.float32)
    old_scale = jnp.transpose(jnp.exp(log_norm - merged), (0, 2, 1))[..., None]
    new_scale = jnp.transpose(jnp.exp(row_max - merged), (0, 2, 1))[..., None]
    return (merged, outputs * old_scale + weighted * new_scale)


def doubling_gather(block, axis, bits):
    index = lax.axis_index(axis)
    size = lax.axis_size(axis)
    gathered = block[None]
    for bit in bits:
        stride = 1 << bit
        received = lax.ppermute(gathered, axis, [(i, i ^ stride) for i in range(size)])
        low = (index // stride) % 2 == 0
        gathered = jnp.where(low, jnp.stack([gathered, received]), jnp.stack([received, gathered]))
    order = sorted(range(len(bits)), key=lambda axis_pos: -bits[len(bits) - 1 - axis_pos])
    gathered = jnp.transpose(gathered, order + list(range(len(bits), gathered.ndim)))
    return gathered.reshape((size,) + block.shape)


def grouped_gather(block, axis, outer, inner):
    inner_groups = [[g * inner + i for i in range(inner)] for g in range(outer)]
    outer_groups = [[i * inner + g for i in range(outer)] for g in range(inner)]
    spread = jnp.broadcast_to(block[None], (inner,) + block.shape)
    near = lax.all_to_all(spread, axis, 0, 0, axis_index_groups=inner_groups)
    spread = jnp.broadcast_to(near[None], (outer,) + near.shape)
    far = lax.all_to_all(spread, axis, 0, 0, axis_index_groups=outer_groups)
    return far.reshape((outer * inner,) + block.shape)


def chip_position(row, col):
    return ((col // 2) % 4, row % 4, 8 * (col // 8) + row // 4)


def hop_count(source, target):
    sizes = (4, 4, 16)
    total = 0
    for a, b, n in zip(source, target, sizes):
        d = abs(a - b) % n
        total += min(d, n - d)
    return total


def assignment(cost):
    n = len(cost)
    u = [0] * (n + 1)
    v = [0] * (n + 1)
    match = [0] * (n + 1)
    way = [0] * (n + 1)
    for i in range(1, n + 1):
        match[0] = i
        j0 = 0
        minv = [float("inf")] * (n + 1)
        used = [False] * (n + 1)
        while True:
            used[j0] = True
            i0 = match[j0]
            delta = float("inf")
            j1 = 0
            for j in range(1, n + 1):
                if not used[j]:
                    cur = cost[i0 - 1][j - 1] - u[i0] - v[j]
                    if cur < minv[j]:
                        minv[j] = cur
                        way[j] = j0
                    if minv[j] < delta:
                        delta = minv[j]
                        j1 = j
            for j in range(n + 1):
                if used[j]:
                    u[match[j]] += delta
                    v[j] -= delta
                else:
                    minv[j] -= delta
            j0 = j1
            if match[j0] == 0:
                break
        while True:
            j1 = way[j0]
            match[j0] = match[j1]
            j0 = j1
            if j0 == 0:
                break
    chosen = [0] * n
    for j in range(1, n + 1):
        chosen[match[j] - 1] = j - 1
    return chosen


def route(source, target):
    sizes = (4, 4, 16)
    routes = []
    for order in itertools.permutations(range(3)):
        cur = list(source)
        links = []
        for dim in order:
            n = sizes[dim]
            delta = (target[dim] - cur[dim]) % n
            step = 1 if delta <= n - delta else -1
            while cur[dim] != target[dim]:
                links.append((order, tuple(cur), dim, step))
                cur[dim] = (cur[dim] + step) % n
        routes.append(links)
    return [link for links in routes for link in links]


def owner_perm(n_row, n_col, groups, sweeps=3):
    load = collections.Counter()
    chosen = {}
    paths = {}
    for _ in range(sweeps):
        for col in range(n_col):
            sources = [(r, cc) for r in range(groups * col, groups * col + groups) for cc in range(n_col)]
            for src, p in chosen.get(col, []):
                for link in paths[(src, p, col)]:
                    load[link] -= 1
            cost = []
            for src in sources:
                row_cost = []
                for p in range(n_row):
                    key = (src, p, col)
                    if key not in paths:
                        paths[key] = route(chip_position(*src), chip_position(p, col))
                    row_cost.append(sum(2 * load[link] + 1 for link in paths[key]))
                cost.append(row_cost)
            chosen[col] = list(zip(sources, assignment(cost)))
            for src, p in chosen[col]:
                for link in paths[(src, p, col)]:
                    load[link] += 1
    return [(src[0] * n_col + src[1], p * n_col + col) for col in range(n_col) for src, p in chosen[col]]


def shards(
    pair_act,
    token_mask,
    step_offset,
    triangle_weight,
    query_weight,
    key_value_weight,
    bias_weight,
    triangle_carry,
    log_carry,
    output_carry,
):
    row_count, col_width, channels = pair_act.shape
    n_row = lax.axis_size("row")
    n_col = lax.axis_size("col")
    groups = col_width // row_count
    row_index = lax.axis_index("row")
    col_index = lax.axis_index("col")
    width = HEADS * HEAD_DIM
    window = STEPS * col_width
    piece = window // n_col

    start = step_offset[0] % n_col
    block_ids = (start + jnp.arange(STEPS, dtype=jnp.int32)) % n_col
    columns = (block_ids[:, None] * col_width + jnp.arange(col_width, dtype=jnp.int32)[None, :]).reshape(-1)
    mask_float = token_mask.astype(jnp.float32)
    key_mask = jnp.take(token_mask, columns)
    key_keep = jnp.take(mask_float, columns)
    row_mask = lax.dynamic_slice_in_dim(mask_float, row_index * row_count, row_count)
    col_mask = lax.dynamic_slice_in_dim(mask_float, col_index * col_width, col_width)

    def in_window(col):
        return (col - start) % n_col < STEPS

    received = lax.ppermute(pair_act, "col", [(i, i ^ 8) for i in range(n_col)])
    held = jnp.where(in_window(col_index), pair_act, received)
    mine_ok = in_window(col_index) | in_window(col_index ^ 8)

    partner = lax.ppermute(held, "row", [(i, i ^ 1) for i in range(n_row)])
    odd = row_index % 2 == 1
    held = jnp.where(odd, jnp.concatenate([partner, held]), jnp.concatenate([held, partner]))

    received = lax.ppermute(held, "col", [(i, i ^ 4) for i in range(n_col)])
    held = jnp.where(mine_ok, held, received)
    received = lax.ppermute(held, "col", [(i, i ^ 2) for i in range(n_col)])
    first = ((col_index - start) % 4) // 2 == 0
    pair = jnp.where(first, jnp.stack([held, received]), jnp.stack([received, held]))
    received = lax.ppermute(pair, "col", [(i, i ^ 1) for i in range(n_col)])
    even = (col_index - start) % 2 == 0
    tiles = jnp.where(even, jnp.stack([pair, received], axis=1), jnp.stack([received, pair], axis=1))
    tiles = tiles.reshape((STEPS,) + held.shape)

    rows_act = lax.dynamic_slice_in_dim(tiles, (row_index % groups) * row_count, row_count, axis=1)
    rows_act = rows_act.transpose(1, 0, 2, 3).reshape(row_count, window, channels)

    perm = owner_perm(n_row, n_col, groups)
    moved = lax.ppermute(tiles, ("row", "col"), perm)
    cols_act = moved.transpose(1, 0, 2, 3).reshape(groups * row_count, window, channels)

    normed = layer_norm(pair_act)
    queries = (project(normed, query_weight) * (1.0 / math.sqrt(HEAD_DIM))).astype(jnp.bfloat16)
    queries = queries.reshape(row_count, col_width, HEADS, HEAD_DIM)

    rows_normed = layer_norm(rows_act)
    cols_normed = layer_norm(cols_act)
    left = gate_pair(
        project(rows_normed, triangle_weight[:, : 2 * TRI_DIM]),
        row_mask[:, None, None] * key_keep[None, :, None],
    )
    right = gate_pair(
        project(cols_normed, triangle_weight[:, 2 * TRI_DIM :]),
        col_mask[:, None, None] * key_keep[None, :, None],
    )
    key_value = project(rows_normed, key_value_weight).astype(jnp.bfloat16)
    pair_bias = jnp.transpose(project(cols_normed, bias_weight).astype(jnp.bfloat16), (2, 0, 1))

    triangle_sums = triangle_carry + jnp.einsum(
        "ikc,jkc->ijc", left, right, preferred_element_type=jnp.float32
    )

    keys = key_value[..., :width].reshape(row_count, window, HEADS, HEAD_DIM)
    values = key_value[..., width:].reshape(row_count, window, HEADS, HEAD_DIM)
    scores = jnp.einsum("ijhd,ikhd->ihjk", queries, keys, preferred_element_type=jnp.float32)
    scores = scores + pair_bias[None].astype(jnp.float32)
    scores = jnp.where(key_mask[None, None, None, :] == 1, scores, -1000000000.0)

    log_norm = jnp.transpose(log_carry, (1, 0, 2))
    outputs = output_carry.reshape(row_count, col_width, HEADS, HEAD_DIM)
    for window_step in range(STEPS):
        lo = window_step * col_width
        hi = lo + col_width
        log_norm, outputs = softmax_merge(scores[..., lo:hi], values[:, lo:hi], log_norm, outputs)
    return (
        triangle_sums,
        jnp.transpose(log_norm, (1, 0, 2)),
        outputs.reshape(row_count, col_width, width),
    )


def solution(mesh):
    return jax.shard_map(
        shards,
        mesh=mesh,
        in_specs=(
            P("row", "col", None),
            P(),
            P(),
            P(),
            P(),
            P(),
            P(),
            P("row", "col", None),
            P(None, "row", "col"),
            P("row", "col", None),
        ),
        out_specs=(P("row", "col", None), P(None, "row", "col"), P("row", "col", None)),
        check_vma=False,
    )
```

```python
import collections
import itertools
import math

import jax
import jax.numpy as jnp
from jax import lax
from jax.sharding import PartitionSpec as P

TRI_DIM = 128
HEADS = 4
HEAD_DIM = 32
STEPS = 4
COL_BITS = (3, 2, 1, 0)
ROW_BITS = (4, 3, 1, 2, 0)
Y_SIZE = 4


def layer_norm(values):
    floats = values.astype(jnp.float32)
    average = jnp.mean(floats, axis=-1, keepdims=True)
    centred = floats - average
    variance = jnp.mean(centred * centred, axis=-1, keepdims=True)
    return (centred * lax.rsqrt(variance + 1e-05)).astype(jnp.bfloat16)


def project(normed, weight):
    flattened = normed.reshape(-1, normed.shape[-1])
    result = jnp.dot(flattened, weight, preferred_element_type=jnp.float32)
    return result.reshape(normed.shape[:-1] + (weight.shape[1],))


def gate_pair(projected, pair_keep):
    gate_part = projected[..., :TRI_DIM]
    value_part = projected[..., TRI_DIM : 2 * TRI_DIM]
    return (jax.nn.sigmoid(gate_part) * value_part * pair_keep).astype(jnp.bfloat16)


def softmax_merge(scores, values, log_norm, outputs):
    row_max = jnp.max(scores, axis=-1)
    shifted = jnp.exp(scores - row_max[..., None])
    block_log = row_max + jnp.log(jnp.sum(shifted, axis=-1))
    merged = jnp.logaddexp(log_norm, block_log)
    weights = shifted.astype(jnp.bfloat16)
    weighted = jnp.einsum("ihjk,ikhd->ijhd", weights, values, preferred_element_type=jnp.float32)
    old_scale = jnp.transpose(jnp.exp(log_norm - merged), (0, 2, 1))[..., None]
    new_scale = jnp.transpose(jnp.exp(row_max - merged), (0, 2, 1))[..., None]
    return (merged, outputs * old_scale + weighted * new_scale)


def doubling_gather(block, axis, bits):
    index = lax.axis_index(axis)
    size = lax.axis_size(axis)
    gathered = block[None]
    for bit in bits:
        stride = 1 << bit
        received = lax.ppermute(gathered, axis, [(i, i ^ stride) for i in range(size)])
        low = (index // stride) % 2 == 0
        gathered = jnp.where(low, jnp.stack([gathered, received]), jnp.stack([received, gathered]))
    order = sorted(range(len(bits)), key=lambda axis_pos: -bits[len(bits) - 1 - axis_pos])
    gathered = jnp.transpose(gathered, order + list(range(len(bits), gathered.ndim)))
    return gathered.reshape((size,) + block.shape)


def grouped_gather(block, axis, outer, inner):
    inner_groups = [[g * inner + i for i in range(inner)] for g in range(outer)]
    outer_groups = [[i * inner + g for i in range(outer)] for g in range(inner)]
    spread = jnp.broadcast_to(block[None], (inner,) + block.shape)
    near = lax.all_to_all(spread, axis, 0, 0, axis_index_groups=inner_groups)
    spread = jnp.broadcast_to(near[None], (outer,) + near.shape)
    far = lax.all_to_all(spread, axis, 0, 0, axis_index_groups=outer_groups)
    return far.reshape((outer * inner,) + block.shape)


def chip_position(row, col):
    return ((col // 2) % 4, row % 4, 8 * (col // 8) + row // 4)


def hop_count(source, target):
    sizes = (4, 4, 16)
    total = 0
    for a, b, n in zip(source, target, sizes):
        d = abs(a - b) % n
        total += min(d, n - d)
    return total


def assignment(cost):
    n = len(cost)
    u = [0] * (n + 1)
    v = [0] * (n + 1)
    match = [0] * (n + 1)
    way = [0] * (n + 1)
    for i in range(1, n + 1):
        match[0] = i
        j0 = 0
        minv = [float("inf")] * (n + 1)
        used = [False] * (n + 1)
        while True:
            used[j0] = True
            i0 = match[j0]
            delta = float("inf")
            j1 = 0
            for j in range(1, n + 1):
                if not used[j]:
                    cur = cost[i0 - 1][j - 1] - u[i0] - v[j]
                    if cur < minv[j]:
                        minv[j] = cur
                        way[j] = j0
                    if minv[j] < delta:
                        delta = minv[j]
                        j1 = j
            for j in range(n + 1):
                if used[j]:
                    u[match[j]] += delta
                    v[j] -= delta
                else:
                    minv[j] -= delta
            j0 = j1
            if match[j0] == 0:
                break
        while True:
            j1 = way[j0]
            match[j0] = match[j1]
            j0 = j1
            if j0 == 0:
                break
    chosen = [0] * n
    for j in range(1, n + 1):
        chosen[match[j] - 1] = j - 1
    return chosen


def route(source, target):
    sizes = (4, 4, 16)
    routes = []
    for order in itertools.permutations(range(3)):
        cur = list(source)
        links = []
        for dim in order:
            n = sizes[dim]
            delta = (target[dim] - cur[dim]) % n
            step = 1 if delta <= n - delta else -1
            while cur[dim] != target[dim]:
                links.append((order, tuple(cur), dim, step))
                cur[dim] = (cur[dim] + step) % n
        routes.append(links)
    return [link for links in routes for link in links]


def owner_perm(n_row, n_col, groups, sweeps=3):
    load = collections.Counter()
    chosen = {}
    paths = {}
    for _ in range(sweeps):
        for col in range(n_col):
            sources = [(r, cc) for r in range(groups * col, groups * col + groups) for cc in range(n_col)]
            for src, p in chosen.get(col, []):
                for link in paths[(src, p, col)]:
                    load[link] -= 1
            cost = []
            for src in sources:
                row_cost = []
                for p in range(n_row):
                    key = (src, p, col)
                    if key not in paths:
                        paths[key] = route(chip_position(*src), chip_position(p, col))
                    row_cost.append(sum(2 * load[link] + 1 for link in paths[key]))
                cost.append(row_cost)
            chosen[col] = list(zip(sources, assignment(cost)))
            for src, p in chosen[col]:
                for link in paths[(src, p, col)]:
                    load[link] += 1
    return [(src[0] * n_col + src[1], p * n_col + col) for col in range(n_col) for src, p in chosen[col]]


def shards(
    pair_act,
    token_mask,
    step_offset,
    triangle_weight,
    query_weight,
    key_value_weight,
    bias_weight,
    triangle_carry,
    log_carry,
    output_carry,
):
    row_count, col_width, channels = pair_act.shape
    n_row = lax.axis_size("row")
    n_col = lax.axis_size("col")
    groups = col_width // row_count
    row_index = lax.axis_index("row")
    col_index = lax.axis_index("col")
    width = HEADS * HEAD_DIM
    window = STEPS * col_width
    piece = window // n_col

    start = step_offset[0] % n_col
    block_ids = (start + jnp.arange(STEPS, dtype=jnp.int32)) % n_col
    columns = (block_ids[:, None] * col_width + jnp.arange(col_width, dtype=jnp.int32)[None, :]).reshape(-1)
    mask_float = token_mask.astype(jnp.float32)
    key_mask = jnp.take(token_mask, columns)
    key_keep = jnp.take(mask_float, columns)
    row_mask = lax.dynamic_slice_in_dim(mask_float, row_index * row_count, row_count)
    col_mask = lax.dynamic_slice_in_dim(mask_float, col_index * col_width, col_width)

    def in_window(col):
        return (col - start) % n_col < STEPS

    received = lax.ppermute(pair_act, "col", [(i, i ^ 8) for i in range(n_col)])
    held = jnp.where(in_window(col_index), pair_act, received)
    mine_ok = in_window(col_index) | in_window(col_index ^ 8)

    partner = lax.ppermute(held, "row", [(i, i ^ 1) for i in range(n_row)])
    odd = row_index % 2 == 1
    held = jnp.where(odd, jnp.concatenate([partner, held]), jnp.concatenate([held, partner]))

    received = lax.ppermute(held, "col", [(i, i ^ 4) for i in range(n_col)])
    held = jnp.where(mine_ok, held, received)
    received = lax.ppermute(held, "col", [(i, i ^ 2) for i in range(n_col)])
    first = ((col_index - start) % 4) // 2 == 0
    pair = jnp.where(first, jnp.stack([held, received]), jnp.stack([received, held]))
    received = lax.ppermute(pair, "col", [(i, i ^ 1) for i in range(n_col)])
    even = (col_index - start) % 2 == 0
    tiles = jnp.where(even, jnp.stack([pair, received], axis=1), jnp.stack([received, pair], axis=1))
    tiles = tiles.reshape((STEPS,) + held.shape)

    rows_act = lax.dynamic_slice_in_dim(tiles, (row_index % groups) * row_count, row_count, axis=1)
    rows_act = rows_act.transpose(1, 0, 2, 3).reshape(row_count, window, channels)

    perm = owner_perm(n_row, n_col, groups)
    moved = lax.ppermute(tiles, ("row", "col"), perm)
    cols_act = moved

    normed = layer_norm(pair_act)
    queries = (project(normed, query_weight) * (1.0 / math.sqrt(HEAD_DIM))).astype(jnp.bfloat16)
    queries = queries.reshape(row_count, col_width, HEADS, HEAD_DIM)

    rows_normed = layer_norm(rows_act)
    cols_normed = layer_norm(cols_act)
    left = gate_pair(
        project(rows_normed, triangle_weight[:, : 2 * TRI_DIM]),
        row_mask[:, None, None] * key_keep[None, :, None],
    )
    right = gate_pair(
        project(cols_normed, triangle_weight[:, 2 * TRI_DIM :]),
        col_mask[None, :, None, None] * key_keep.reshape(STEPS, 1, col_width, 1),
    )
    key_value = project(rows_normed, key_value_weight).astype(jnp.bfloat16)
    pair_bias = jnp.transpose(project(cols_normed, bias_weight).astype(jnp.bfloat16), (3, 1, 0, 2))
    pair_bias = pair_bias.reshape(HEADS, col_width, window)

    triangle_sums = triangle_carry + jnp.einsum(
        "itkc,tjkc->ijc",
        left.reshape(row_count, STEPS, col_width, TRI_DIM),
        right,
        preferred_element_type=jnp.float32,
    )

    keys = key_value[..., :width].reshape(row_count, window, HEADS, HEAD_DIM)
    values = key_value[..., width:].reshape(row_count, window, HEADS, HEAD_DIM)
    scores = jnp.einsum("ijhd,ikhd->ihjk", queries, keys, preferred_element_type=jnp.float32)
    scores = scores + pair_bias[None].astype(jnp.float32)
    scores = jnp.where(key_mask[None, None, None, :] == 1, scores, -1000000000.0)

    log_norm = jnp.transpose(log_carry, (1, 0, 2))
    outputs = output_carry.reshape(row_count, col_width, HEADS, HEAD_DIM)
    for window_step in range(STEPS):
        lo = window_step * col_width
        hi = lo + col_width
        log_norm, outputs = softmax_merge(scores[..., lo:hi], values[:, lo:hi], log_norm, outputs)
    return (
        triangle_sums,
        jnp.transpose(log_norm, (1, 0, 2)),
        outputs.reshape(row_count, col_width, width),
    )


def solution(mesh):
    return jax.shard_map(
        shards,
        mesh=mesh,
        in_specs=(
            P("row", "col", None),
            P(),
            P(),
            P(),
            P(),
            P(),
            P(),
            P("row", "col", None),
            P(None, "row", "col"),
            P("row", "col", None),
        ),
        out_specs=(P("row", "col", None), P(None, "row", "col"), P("row", "col", None)),
        check_vma=False,
    )
```

```python
import collections
import itertools
import math

import jax
import numpy as np
import jax.numpy as jnp
from jax import lax
from jax.sharding import PartitionSpec as P

TRI_DIM = 128
HEADS = 4
HEAD_DIM = 32
STEPS = 4
COL_BITS = (3, 2, 1, 0)
ROW_BITS = (4, 3, 1, 2, 0)
Y_SIZE = 4


def layer_norm(values):
    floats = values.astype(jnp.float32)
    average = jnp.mean(floats, axis=-1, keepdims=True)
    centred = floats - average
    variance = jnp.mean(centred * centred, axis=-1, keepdims=True)
    return (centred * lax.rsqrt(variance + 1e-05)).astype(jnp.bfloat16)


def project(normed, weight):
    flattened = normed.reshape(-1, normed.shape[-1])
    result = jnp.dot(flattened, weight, preferred_element_type=jnp.float32)
    return result.reshape(normed.shape[:-1] + (weight.shape[1],))


def gate_pair(projected, pair_keep):
    gate_part = projected[..., :TRI_DIM]
    value_part = projected[..., TRI_DIM : 2 * TRI_DIM]
    return (jax.nn.sigmoid(gate_part) * value_part * pair_keep).astype(jnp.bfloat16)


def softmax_merge(scores, values, log_norm, outputs):
    row_max = jnp.max(scores, axis=-1)
    shifted = jnp.exp(scores - row_max[..., None])
    block_log = row_max + jnp.log(jnp.sum(shifted, axis=-1))
    merged = jnp.logaddexp(log_norm, block_log)
    weights = shifted.astype(jnp.bfloat16)
    weighted = jnp.einsum("ihjk,ikhd->ijhd", weights, values, preferred_element_type=jnp.float32)
    old_scale = jnp.transpose(jnp.exp(log_norm - merged), (0, 2, 1))[..., None]
    new_scale = jnp.transpose(jnp.exp(row_max - merged), (0, 2, 1))[..., None]
    return (merged, outputs * old_scale + weighted * new_scale)


def doubling_gather(block, axis, bits):
    index = lax.axis_index(axis)
    size = lax.axis_size(axis)
    gathered = block[None]
    for bit in bits:
        stride = 1 << bit
        received = lax.ppermute(gathered, axis, [(i, i ^ stride) for i in range(size)])
        low = (index // stride) % 2 == 0
        gathered = jnp.where(low, jnp.stack([gathered, received]), jnp.stack([received, gathered]))
    order = sorted(range(len(bits)), key=lambda axis_pos: -bits[len(bits) - 1 - axis_pos])
    gathered = jnp.transpose(gathered, order + list(range(len(bits), gathered.ndim)))
    return gathered.reshape((size,) + block.shape)


def grouped_gather(block, axis, outer, inner):
    inner_groups = [[g * inner + i for i in range(inner)] for g in range(outer)]
    outer_groups = [[i * inner + g for i in range(outer)] for g in range(inner)]
    spread = jnp.broadcast_to(block[None], (inner,) + block.shape)
    near = lax.all_to_all(spread, axis, 0, 0, axis_index_groups=inner_groups)
    spread = jnp.broadcast_to(near[None], (outer,) + near.shape)
    far = lax.all_to_all(spread, axis, 0, 0, axis_index_groups=outer_groups)
    return far.reshape((outer * inner,) + block.shape)


def chip_position(row, col):
    return ((col // 2) % 4, row % 4, 8 * (col // 8) + row // 4)


def hop_count(source, target):
    sizes = (4, 4, 16)
    total = 0
    for a, b, n in zip(source, target, sizes):
        d = abs(a - b) % n
        total += min(d, n - d)
    return total


def assignment(cost):
    n = len(cost)
    u = [0] * (n + 1)
    v = [0] * (n + 1)
    match = [0] * (n + 1)
    way = [0] * (n + 1)
    for i in range(1, n + 1):
        match[0] = i
        j0 = 0
        minv = [float("inf")] * (n + 1)
        used = [False] * (n + 1)
        while True:
            used[j0] = True
            i0 = match[j0]
            delta = float("inf")
            j1 = 0
            for j in range(1, n + 1):
                if not used[j]:
                    cur = cost[i0 - 1][j - 1] - u[i0] - v[j]
                    if cur < minv[j]:
                        minv[j] = cur
                        way[j] = j0
                    if minv[j] < delta:
                        delta = minv[j]
                        j1 = j
            for j in range(n + 1):
                if used[j]:
                    u[match[j]] += delta
                    v[j] -= delta
                else:
                    minv[j] -= delta
            j0 = j1
            if match[j0] == 0:
                break
        while True:
            j1 = way[j0]
            match[j0] = match[j1]
            j0 = j1
            if j0 == 0:
                break
    chosen = [0] * n
    for j in range(1, n + 1):
        chosen[match[j] - 1] = j - 1
    return chosen


def route(source, target):
    sizes = (4, 4, 16)
    routes = []
    for order in itertools.permutations(range(3)):
        cur = list(source)
        links = []
        for dim in order:
            n = sizes[dim]
            delta = (target[dim] - cur[dim]) % n
            step = 1 if delta <= n - delta else -1
            while cur[dim] != target[dim]:
                links.append((order, tuple(cur), dim, step))
                cur[dim] = (cur[dim] + step) % n
        routes.append(links)
    return [link for links in routes for link in links]


def owner_perm(n_row, n_col, groups, sweeps=3):
    load = collections.Counter()
    chosen = {}
    paths = {}
    for _ in range(sweeps):
        for col in range(n_col):
            sources = [(r, cc) for r in range(groups * col, groups * col + groups) for cc in range(n_col)]
            for src, p in chosen.get(col, []):
                for link in paths[(src, p, col)]:
                    load[link] -= 1
            cost = []
            for src in sources:
                row_cost = []
                for p in range(n_row):
                    key = (src, p, col)
                    if key not in paths:
                        paths[key] = route(chip_position(*src), chip_position(p, col))
                    row_cost.append(sum(2 * load[link] + 1 for link in paths[key]))
                cost.append(row_cost)
            chosen[col] = list(zip(sources, assignment(cost)))
            for src, p in chosen[col]:
                for link in paths[(src, p, col)]:
                    load[link] += 1
    return [(src[0] * n_col + src[1], p * n_col + col) for col in range(n_col) for src, p in chosen[col]]


def shards(
    pair_act,
    token_mask,
    step_offset,
    triangle_weight,
    query_weight,
    key_value_weight,
    bias_weight,
    triangle_carry,
    log_carry,
    output_carry,
):
    row_count, col_width, channels = pair_act.shape
    n_row = lax.axis_size("row")
    n_col = lax.axis_size("col")
    groups = col_width // row_count
    row_index = lax.axis_index("row")
    col_index = lax.axis_index("col")
    width = HEADS * HEAD_DIM
    window = STEPS * col_width
    piece = window // n_col

    start = step_offset[0] % n_col
    block_ids = (start + jnp.arange(STEPS, dtype=jnp.int32)) % n_col
    columns = (block_ids[:, None] * col_width + jnp.arange(col_width, dtype=jnp.int32)[None, :]).reshape(-1)
    mask_float = token_mask.astype(jnp.float32)
    key_mask = jnp.take(token_mask, columns)
    key_keep = jnp.take(mask_float, columns)
    row_mask = lax.dynamic_slice_in_dim(mask_float, row_index * row_count, row_count)
    col_mask = lax.dynamic_slice_in_dim(mask_float, col_index * col_width, col_width)

    def in_window(col):
        return (col - start) % n_col < STEPS

    received = lax.ppermute(pair_act, "col", [(i, i ^ 8) for i in range(n_col)])
    held = jnp.where(in_window(col_index), pair_act, received)
    mine_ok = in_window(col_index) | in_window(col_index ^ 8)

    partner = lax.ppermute(held, "row", [(i, i ^ 1) for i in range(n_row)])
    odd = row_index % 2 == 1
    held = jnp.where(odd, jnp.concatenate([partner, held]), jnp.concatenate([held, partner]))

    received = lax.ppermute(held, "col", [(i, i ^ 4) for i in range(n_col)])
    held = jnp.where(mine_ok, held, received)
    received = lax.ppermute(held, "col", [(i, i ^ 2) for i in range(n_col)])
    first = ((col_index - start) % 4) // 2 == 0
    pair = jnp.where(first, jnp.stack([held, received]), jnp.stack([received, held]))
    received = lax.ppermute(pair, "col", [(i, i ^ 1) for i in range(n_col)])
    even = (col_index - start) % 2 == 0
    tiles = jnp.where(even, jnp.stack([pair, received], axis=1), jnp.stack([received, pair], axis=1))
    tiles = tiles.reshape((STEPS,) + held.shape)

    rows_act = lax.dynamic_slice_in_dim(tiles, (row_index % groups) * row_count, row_count, axis=1)
    rows_act = rows_act.transpose(1, 0, 2, 3).reshape(row_count, window, channels)

    perm = owner_perm(n_row, n_col, groups)
    half_of = np.zeros(n_row * n_col, np.int32)
    for src, dst in perm:
        half_of[src] = (dst // n_col) % groups
    half = jnp.asarray(half_of)[row_index * n_col + col_index]
    sent = lax.dynamic_slice_in_dim(tiles, half * row_count, row_count, axis=1)
    got = lax.ppermute(sent, ("row", "col"), perm)
    other = lax.ppermute(got, "row", [(i, i ^ 1) for i in range(n_row)])
    moved = jnp.where(odd, jnp.concatenate([other, got], axis=1), jnp.concatenate([got, other], axis=1))
    cols_act = moved.transpose(1, 0, 2, 3).reshape(groups * row_count, window, channels)

    normed = layer_norm(pair_act)
    queries = (project(normed, query_weight) * (1.0 / math.sqrt(HEAD_DIM))).astype(jnp.bfloat16)
    queries = queries.reshape(row_count, col_width, HEADS, HEAD_DIM)

    rows_normed = layer_norm(rows_act)
    cols_normed = layer_norm(cols_act)
    left = gate_pair(
        project(rows_normed, triangle_weight[:, : 2 * TRI_DIM]),
        row_mask[:, None, None] * key_keep[None, :, None],
    )
    right = gate_pair(
        project(cols_normed, triangle_weight[:, 2 * TRI_DIM :]),
        col_mask[:, None, None] * key_keep[None, :, None],
    )
    key_value = project(rows_normed, key_value_weight).astype(jnp.bfloat16)
    pair_bias = jnp.transpose(project(cols_normed, bias_weight).astype(jnp.bfloat16), (2, 0, 1))

    triangle_sums = triangle_carry + jnp.einsum(
        "ikc,jkc->ijc", left, right, preferred_element_type=jnp.float32
    )

    keys = key_value[..., :width].reshape(row_count, window, HEADS, HEAD_DIM)
    values = key_value[..., width:].reshape(row_count, window, HEADS, HEAD_DIM)
    scores = jnp.einsum("ijhd,ikhd->ihjk", queries, keys, preferred_element_type=jnp.float32)
    scores = scores + pair_bias[None].astype(jnp.float32)
    scores = jnp.where(key_mask[None, None, None, :] == 1, scores, -1000000000.0)

    log_norm = jnp.transpose(log_carry, (1, 0, 2))
    outputs = output_carry.reshape(row_count, col_width, HEADS, HEAD_DIM)
    for window_step in range(STEPS):
        lo = window_step * col_width
        hi = lo + col_width
        log_norm, outputs = softmax_merge(scores[..., lo:hi], values[:, lo:hi], log_norm, outputs)
    return (
        triangle_sums,
        jnp.transpose(log_norm, (1, 0, 2)),
        outputs.reshape(row_count, col_width, width),
    )


def solution(mesh):
    return jax.shard_map(
        shards,
        mesh=mesh,
        in_specs=(
            P("row", "col", None),
            P(),
            P(),
            P(),
            P(),
            P(),
            P(),
            P("row", "col", None),
            P(None, "row", "col"),
            P("row", "col", None),
        ),
        out_specs=(P("row", "col", None), P(None, "row", "col"), P("row", "col", None)),
        check_vma=False,
    )
```

```python
import collections
import itertools
import math

import jax
import jax.numpy as jnp
from jax import lax
from jax.sharding import PartitionSpec as P

TRI_DIM = 128
HEADS = 4
HEAD_DIM = 32
STEPS = 4
COL_BITS = (3, 2, 1, 0)
ROW_BITS = (4, 3, 1, 2, 0)
Y_SIZE = 4


def layer_norm(values):
    floats = values.astype(jnp.float32)
    average = jnp.mean(floats, axis=-1, keepdims=True)
    centred = floats - average
    variance = jnp.mean(centred * centred, axis=-1, keepdims=True)
    return (centred * lax.rsqrt(variance + 1e-05)).astype(jnp.bfloat16)


def project(normed, weight):
    flattened = normed.reshape(-1, normed.shape[-1])
    result = jnp.dot(flattened, weight, preferred_element_type=jnp.float32)
    return result.reshape(normed.shape[:-1] + (weight.shape[1],))


def gate_pair(projected, pair_keep):
    gate_part = projected[..., :TRI_DIM]
    value_part = projected[..., TRI_DIM : 2 * TRI_DIM]
    return (jax.nn.sigmoid(gate_part) * value_part * pair_keep).astype(jnp.bfloat16)


def softmax_merge(scores, values, log_norm, outputs):
    row_max = jnp.max(scores, axis=-1)
    shifted = jnp.exp(scores - row_max[..., None])
    block_log = row_max + jnp.log(jnp.sum(shifted, axis=-1))
    merged = jnp.logaddexp(log_norm, block_log)
    weights = shifted.astype(jnp.bfloat16)
    weighted = jnp.einsum("ihjk,ikhd->ijhd", weights, values, preferred_element_type=jnp.float32)
    old_scale = jnp.transpose(jnp.exp(log_norm - merged), (0, 2, 1))[..., None]
    new_scale = jnp.transpose(jnp.exp(row_max - merged), (0, 2, 1))[..., None]
    return (merged, outputs * old_scale + weighted * new_scale)


def doubling_gather(block, axis, bits):
    index = lax.axis_index(axis)
    size = lax.axis_size(axis)
    gathered = block[None]
    for bit in bits:
        stride = 1 << bit
        received = lax.ppermute(gathered, axis, [(i, i ^ stride) for i in range(size)])
        low = (index // stride) % 2 == 0
        gathered = jnp.where(low, jnp.stack([gathered, received]), jnp.stack([received, gathered]))
    order = sorted(range(len(bits)), key=lambda axis_pos: -bits[len(bits) - 1 - axis_pos])
    gathered = jnp.transpose(gathered, order + list(range(len(bits), gathered.ndim)))
    return gathered.reshape((size,) + block.shape)


def grouped_gather(block, axis, outer, inner):
    inner_groups = [[g * inner + i for i in range(inner)] for g in range(outer)]
    outer_groups = [[i * inner + g for i in range(outer)] for g in range(inner)]
    spread = jnp.broadcast_to(block[None], (inner,) + block.shape)
    near = lax.all_to_all(spread, axis, 0, 0, axis_index_groups=inner_groups)
    spread = jnp.broadcast_to(near[None], (outer,) + near.shape)
    far = lax.all_to_all(spread, axis, 0, 0, axis_index_groups=outer_groups)
    return far.reshape((outer * inner,) + block.shape)


def chip_position(row, col):
    return ((col // 2) % 4, row % 4, 8 * (col // 8) + row // 4)


def hop_count(source, target):
    sizes = (4, 4, 16)
    total = 0
    for a, b, n in zip(source, target, sizes):
        d = abs(a - b) % n
        total += min(d, n - d)
    return total


def assignment(cost):
    n = len(cost)
    u = [0] * (n + 1)
    v = [0] * (n + 1)
    match = [0] * (n + 1)
    way = [0] * (n + 1)
    for i in range(1, n + 1):
        match[0] = i
        j0 = 0
        minv = [float("inf")] * (n + 1)
        used = [False] * (n + 1)
        while True:
            used[j0] = True
            i0 = match[j0]
            delta = float("inf")
            j1 = 0
            for j in range(1, n + 1):
                if not used[j]:
                    cur = cost[i0 - 1][j - 1] - u[i0] - v[j]
                    if cur < minv[j]:
                        minv[j] = cur
                        way[j] = j0
                    if minv[j] < delta:
                        delta = minv[j]
                        j1 = j
            for j in range(n + 1):
                if used[j]:
                    u[match[j]] += delta
                    v[j] -= delta
                else:
                    minv[j] -= delta
            j0 = j1
            if match[j0] == 0:
                break
        while True:
            j1 = way[j0]
            match[j0] = match[j1]
            j0 = j1
            if j0 == 0:
                break
    chosen = [0] * n
    for j in range(1, n + 1):
        chosen[match[j] - 1] = j - 1
    return chosen


def route(source, target):
    sizes = (4, 4, 16)
    routes = []
    for order in itertools.permutations(range(3)):
        cur = list(source)
        links = []
        for dim in order:
            n = sizes[dim]
            delta = (target[dim] - cur[dim]) % n
            step = 1 if delta <= n - delta else -1
            while cur[dim] != target[dim]:
                links.append((order, tuple(cur), dim, step))
                cur[dim] = (cur[dim] + step) % n
        routes.append(links)
    return [link for links in routes for link in links]


def owner_perm(n_row, n_col, groups, sweeps=3):
    load = collections.Counter()
    chosen = {}
    paths = {}
    for _ in range(sweeps):
        for col in range(n_col):
            sources = [(r, cc) for r in range(groups * col, groups * col + groups) for cc in range(n_col)]
            for src, p in chosen.get(col, []):
                for link in paths[(src, p, col)]:
                    load[link] -= 1
            cost = []
            for src in sources:
                row_cost = []
                for p in range(n_row):
                    key = (src, p, col)
                    if key not in paths:
                        paths[key] = route(chip_position(*src), chip_position(p, col))
                    mismatch = (p - src[0]) % groups != 0
                    row_cost.append(sum(2 * load[link] + 1 for link in paths[key]) + mismatch * 10**6)
                cost.append(row_cost)
            chosen[col] = list(zip(sources, assignment(cost)))
            for src, p in chosen[col]:
                for link in paths[(src, p, col)]:
                    load[link] += 1
    return [(src[0] * n_col + src[1], p * n_col + col) for col in range(n_col) for src, p in chosen[col]]


def shards(
    pair_act,
    token_mask,
    step_offset,
    triangle_weight,
    query_weight,
    key_value_weight,
    bias_weight,
    triangle_carry,
    log_carry,
    output_carry,
):
    row_count, col_width, channels = pair_act.shape
    n_row = lax.axis_size("row")
    n_col = lax.axis_size("col")
    groups = col_width // row_count
    row_index = lax.axis_index("row")
    col_index = lax.axis_index("col")
    width = HEADS * HEAD_DIM
    window = STEPS * col_width
    piece = window // n_col

    start = step_offset[0] % n_col
    block_ids = (start + jnp.arange(STEPS, dtype=jnp.int32)) % n_col
    columns = (block_ids[:, None] * col_width + jnp.arange(col_width, dtype=jnp.int32)[None, :]).reshape(-1)
    mask_float = token_mask.astype(jnp.float32)
    key_mask = jnp.take(token_mask, columns)
    key_keep = jnp.take(mask_float, columns)
    row_mask = lax.dynamic_slice_in_dim(mask_float, row_index * row_count, row_count)
    col_mask = lax.dynamic_slice_in_dim(mask_float, col_index * col_width, col_width)

    def in_window(col):
        return (col - start) % n_col < STEPS

    received = lax.ppermute(pair_act, "col", [(i, i ^ 8) for i in range(n_col)])
    held = jnp.where(in_window(col_index), pair_act, received)
    mine_ok = in_window(col_index) | in_window(col_index ^ 8)

    partner = lax.ppermute(held, "row", [(i, i ^ 1) for i in range(n_row)])
    odd = row_index % 2 == 1
    held = jnp.where(odd, jnp.concatenate([partner, held]), jnp.concatenate([held, partner]))

    received = lax.ppermute(held, "col", [(i, i ^ 4) for i in range(n_col)])
    held = jnp.where(mine_ok, held, received)
    received = lax.ppermute(held, "col", [(i, i ^ 2) for i in range(n_col)])
    first = ((col_index - start) % 4) // 2 == 0
    pair = jnp.where(first, jnp.stack([held, received]), jnp.stack([received, held]))
    received = lax.ppermute(pair, "col", [(i, i ^ 1) for i in range(n_col)])
    even = (col_index - start) % 2 == 0
    tiles = jnp.where(even, jnp.stack([pair, received], axis=1), jnp.stack([received, pair], axis=1))
    tiles = tiles.reshape((STEPS,) + held.shape)

    own_rows = lax.dynamic_slice_in_dim(tiles, (row_index % groups) * row_count, row_count, axis=1)
    rows_act = own_rows.transpose(1, 0, 2, 3).reshape(row_count, window, channels)

    perm = owner_perm(n_row, n_col, groups)
    sent = own_rows
    got = lax.ppermute(sent, ("row", "col"), perm)
    other = lax.ppermute(got, "row", [(i, i ^ 1) for i in range(n_row)])
    moved = jnp.where(odd, jnp.concatenate([other, got], axis=1), jnp.concatenate([got, other], axis=1))
    cols_act = moved.transpose(1, 0, 2, 3).reshape(groups * row_count, window, channels)

    normed = layer_norm(pair_act)
    queries = (project(normed, query_weight) * (1.0 / math.sqrt(HEAD_DIM))).astype(jnp.bfloat16)
    queries = queries.reshape(row_count, col_width, HEADS, HEAD_DIM)

    rows_normed = layer_norm(rows_act)
    cols_normed = layer_norm(cols_act)
    left = gate_pair(
        project(rows_normed, triangle_weight[:, : 2 * TRI_DIM]),
        row_mask[:, None, None] * key_keep[None, :, None],
    )
    right = gate_pair(
        project(cols_normed, triangle_weight[:, 2 * TRI_DIM :]),
        col_mask[:, None, None] * key_keep[None, :, None],
    )
    key_value = project(rows_normed, key_value_weight).astype(jnp.bfloat16)
    pair_bias = jnp.transpose(project(cols_normed, bias_weight).astype(jnp.bfloat16), (2, 0, 1))

    triangle_sums = triangle_carry + jnp.einsum(
        "ikc,jkc->ijc", left, right, preferred_element_type=jnp.float32
    )

    keys = key_value[..., :width].reshape(row_count, window, HEADS, HEAD_DIM)
    values = key_value[..., width:].reshape(row_count, window, HEADS, HEAD_DIM)
    scores = jnp.einsum("ijhd,ikhd->ihjk", queries, keys, preferred_element_type=jnp.float32)
    scores = scores + pair_bias[None].astype(jnp.float32)
    scores = jnp.where(key_mask[None, None, None, :] == 1, scores, -1000000000.0)

    log_norm = jnp.transpose(log_carry, (1, 0, 2))
    outputs = output_carry.reshape(row_count, col_width, HEADS, HEAD_DIM)
    for window_step in range(STEPS):
        lo = window_step * col_width
        hi = lo + col_width
        log_norm, outputs = softmax_merge(scores[..., lo:hi], values[:, lo:hi], log_norm, outputs)
    return (
        triangle_sums,
        jnp.transpose(log_norm, (1, 0, 2)),
        outputs.reshape(row_count, col_width, width),
    )


def solution(mesh):
    return jax.shard_map(
        shards,
        mesh=mesh,
        in_specs=(
            P("row", "col", None),
            P(),
            P(),
            P(),
            P(),
            P(),
            P(),
            P("row", "col", None),
            P(None, "row", "col"),
            P("row", "col", None),
        ),
        out_specs=(P("row", "col", None), P(None, "row", "col"), P("row", "col", None)),
        check_vma=False,
    )
```
